256 devices in a mesh: req: 16 (over x, z_hi, core), tp: 16 (over y, z_lo).
Axes of the slice: x: 4, y: 4, z: 8 (z_hi: 2, z_lo: 4; z = z_hi * 4 + z_lo), core: 2. Of those that a mesh axis runs over, the one named last changes fastest.
Arguments:
- tokens: bfloat16 [16, 512, 3200], P('req', 'tp'), may hold values from -6 to 6
- segments: int32 [16, 512], P('req'), may hold values from -1 to 7, as said below
- norm_gain: float32 [3200], replicated, may hold values from 0.25 to 1.75
- wqkv: bfloat16 [3, 3200, 2048], P(None, None, 'tp'), may hold values from -4 to 4
- qk_gain: float32 [2, 2048], P(None, 'tp'), may hold values from 0.6 to 4
- wproj: bfloat16 [2048, 3200], P('tp'), may hold values from -0.125 to 0.125
- bproj: float32 [3200], P('tp'), may hold values from -3 to 3
- layer_scale: float32 [3200], P('tp'), may hold values from 0.3 to 1.5
- ln_weight: float32 [4, 3200], P(None, 'tp'), may hold values from 0.25 to 1.75
- ln_bias: float32 [4, 3200], P(None, 'tp'), may hold values from -2 to 2
- w_merge: bfloat16 [4, 3200, 3072], P(None, 'tp'), may hold values from -0.0546875 to 0.0546875
- b_merge: float32 [3072], replicated, may hold values from -3 to 3
- owners: int32 [16, 128, 1], P(None, 'tp'), may hold values from 0 to 15; in each aligned block of 8 rows (0 to 7, 8 to 15, ..., all dimensions but the last counted through in order) at most 2 rows name the same one
Outputs:
- lm_inputs: bfloat16 [16, 16, 16, 2, 3072], P('req', None, 'tp')
The draws below stay inside these ranges and needn't reach their ends.
Inputs may be any that keep to these rules, and one draw needn't show every extreme that they name: `segments`: each group's tokens are whole images, each a whole number of blocks of 64 tokens (two patch rows); image numbers start at 0 and never fall; padding tokens (-1) fill the end of a group from a block boundary; some group has no padding and some group has padding. `owners`: among the 8 merged tokens of one device (aligned blocks of one group), at most 2 name the same owner.
All inputs are finite; a program needn't handle non-finite values.
Results may differ from the reference program's by a relative error of at most 0.014.
Values may be sent and summed in bfloat16 or wider, within the bound.
No kernel may reach another device: no remote copies, remote signals or barrier semaphores. Data moves between devices by JAX's collectives and lax.ppermute only.
A program may use at most 64 MiB of HBM per device.

```python
import math
import jax
import jax.numpy as jnp
import numpy as np
from jax import lax

D = 3200
HEADS = 16
HD = 128
PF = 3072
PW = 32
TOK = 512
MERGED = 128
MD = 8
CAP = 2
N_REQ = 16
N_TP = 16


def draw_segments(key, part):
    pair_count = TOK // (2 * PW)
    subkeys = jax.random.split(key, 3)
    full_group = jax.random.randint(subkeys[2], (), 0, N_REQ)
    padded_group = (full_group + 1) % N_REQ
    group_ids = jnp.arange(N_REQ)
    image_cuts = (jax.random.randint(subkeys[0], (N_REQ, pair_count), 0, 3) == 0).astype(jnp.int32)
    image_cuts = jnp.where((group_ids == full_group)[:, None], 1, image_cuts)
    image_cuts = image_cuts.at[:, 0].set(0)
    pair_ids = jnp.cumsum(image_cuts, axis=1)
    kept_pairs = jax.random.randint(subkeys[1], (N_REQ,), (pair_count + 1) // 2, pair_count + 1)
    kept_pairs = jnp.where(group_ids == padded_group, jnp.minimum(kept_pairs, pair_count - 1), kept_pairs)
    kept_pairs = jnp.where(group_ids == full_group, pair_count, kept_pairs)
    live_pairs = jnp.arange(pair_count)[None, :] < kept_pairs[:, None]
    pair_ids = jnp.where(live_pairs, pair_ids, -1)
    return jnp.repeat(pair_ids, 2 * PW, axis=1).astype(jnp.int32)


def draw_wqkv(key, part):
    inner_width = HEADS * HD
    subkeys = jax.random.split(key, 2)
    head_rank = (jnp.arange(inner_width) // HD).astype(jnp.float32)
    rising = jnp.exp(jnp.log(3.0) * head_rank / float(HEADS - 1))
    column_scale = jax.random.uniform(subkeys[1], (3, 1, inner_width), jnp.float32, 0.6, 1.4)
    base_draw = jax.random.normal(subkeys[0], (3, D, inner_width), jnp.float32)
    return (base_draw * column_scale * rising[None, None, :] * D ** (-0.5)).astype(jnp.bfloat16)


def draw_qk_gain(key, part):
    return jax.random.uniform(key, (2, HEADS * HD), jnp.float32, 0.6, 1.4)


def block_levels(key, extent, pieces, smallest, high):
    gain = 1.0
    for axis_at, parts in pieces:
        heights = jax.random.uniform(jax.random.fold_in(jax.random.fold_in(key, 6), axis_at), (parts,), jnp.float32, smallest / len(pieces), high / len(pieces))
        gain = gain * jnp.repeat(jnp.exp(heights), extent[axis_at] // parts).reshape((-1,) + (1,) * (len(extent) - 1 - axis_at))
    return gain


def deal_out(stream_key, own, number, rows, count, top, bound, skew):
    sequence = jax.random.permutation(stream_key, count)
    packed, common = shares(count, rows * top, bound, skew, True), shares(count, rows * top, bound, skew, False)
    places = jnp.arange(count)

    def named(tallies, rotation):
        used = int((tallies > 0).sum())
        fixed = max(1, used // 4)
        passed = fixed + (places - fixed + rotation * (used - fixed)) % max(1, count - fixed)
        return jnp.zeros((count,), jnp.int32).at[sequence[jnp.where(places < fixed, places, passed)]].set(jnp.asarray(tallies, jnp.int32))

    tallies = jnp.where(number % 4 == 0, named(packed, number // 4), named(common, number - number // 4 - 1))
    mixed = jax.random.permutation(jax.random.fold_in(own, 3), count)
    giver, sink = mixed[0:count // 2 * 2:2], mixed[1:count // 2 * 2:2]
    room = jnp.minimum(tallies[giver] - 1, bound - tallies[sink]) // 2
    room = jnp.where((giver == sequence[0]) | (sink == sequence[0]) | (tallies[sink] == 0), 0, jnp.maximum(room, 0))
    passed = jax.random.randint(jax.random.fold_in(own, 4), (count // 2,), 0, 1 << 20) % (room + 1)
    tallies = tallies.at[giver].add(-passed).at[sink].add(passed)
    items = jnp.searchsorted(jnp.cumsum(tallies), jnp.arange(rows * top), side="right").astype(jnp.int32)
    grid = items.reshape(top, rows).T
    grid = grid[jax.random.permutation(jax.random.fold_in(own, 1), rows)]
    rotation = jax.random.randint(jax.random.fold_in(own, 2), (rows, 1), 0, top)
    return jnp.take_along_axis(grid, (jnp.arange(top)[None, :] + rotation) % top, axis=1)


def shares(number_of, total, reach, skew, full):
    portions = [(1 << 20) // math.isqrt(rank ** skew) + 1 for rank in range(1, number_of + 1)]
    largest = reach if full else min(reach, max(-(-total // number_of), total * portions[0] // sum(portions)))
    least = 1 if total - largest >= number_of - 1 else 0
    given, spare = [largest] + [least] * (number_of - 1), total - largest - least * (number_of - 1)
    while spare > 0:
        candidates = [i for i in range(1, number_of) if given[i] < largest] or [i for i in range(1, number_of) if given[i] < reach]
        whole, budget = sum([portions[i] for i in candidates]), spare
        for i in candidates:
            more = min(reach - given[i], max(1, budget * portions[i] // whole), spare)
            given[i] = given[i] + more
            spare = spare - more
    return np.array(given)


def centred(key, extent, deviation, limit, cuts=(), kind=jnp.bfloat16):
    gain = block_levels(key, extent, cuts, -0.22, 0.18) if cuts else 1.0
    drawn = jax.random.normal(key, extent, jnp.float32) * deviation * gain
    return jnp.minimum(jnp.maximum(drawn, -limit), limit).astype(kind)


def setup_inputs(seed: int = 0) -> dict:
    arg_keys = jax.random.split(jax.random.key(seed), 14)
    tokens = centred(arg_keys[0], (N_REQ, TOK, D), 1.0, 6.0, ((0, 16), (1, 16)))
    segments = draw_segments(jax.random.fold_in(arg_keys[13], 71), 0)
    norm_gain = jnp.clip(1.0 + 0.15 * jax.random.normal(arg_keys[2], (D,), jnp.float32), 0.25, 1.75)
    wqkv = draw_wqkv(jax.random.fold_in(arg_keys[13], 71), 0)
    qk_gain = draw_qk_gain(jax.random.fold_in(arg_keys[13], 71), 0)
    wproj = centred(arg_keys[5], (HEADS * HD, D), (HEADS * HD) ** -0.5, 0.125, ((0, 16),))
    bproj = centred(arg_keys[6], (D,), 0.5, 3.0, ((0, 16),), jnp.float32)
    layer_scale = jnp.clip(jnp.exp(math.log(1.5) - 1.60943787 * jax.random.uniform(arg_keys[7], (D,), jnp.float32) ** block_levels(arg_keys[7], (D,), ((0, 16),), -0.2, 0.2)), 0.3, 1.5)
    ln_weight = jnp.clip(1.0 + 0.15 * jax.random.normal(arg_keys[8], (4, D), jnp.float32), 0.25, 1.75)
    ln_bias = centred(arg_keys[9], (4, D), 0.3, 2.0, ((1, 16),), jnp.float32)
    w_merge = centred(arg_keys[10], (4, D, PF), (4 * D) ** -0.5, 0.0546875, ((1, 16),))
    b_merge = centred(arg_keys[11], (PF,), 0.5, 3.0, (), jnp.float32)
    owners_keys = jax.random.split(jax.random.fold_in(arg_keys[12], 1), N_REQ * MERGED // MD)
    owners_turns = jax.random.permutation(jax.random.fold_in(arg_keys[12], 3), N_REQ * MERGED // MD)
    owners = jax.vmap(lambda own, number: deal_out(jax.random.fold_in(arg_keys[12], 2), own, number, MD, N_REQ, 1, CAP, 2))(owners_keys, owners_turns).reshape((N_REQ, MERGED, 1))
    return dict(tokens=tokens, segments=segments, norm_gain=norm_gain, wqkv=wqkv, qk_gain=qk_gain, wproj=wproj, bproj=bproj, layer_scale=layer_scale, ln_weight=ln_weight, ln_bias=ln_bias, w_merge=w_merge, b_merge=b_merge, owners=owners)


EPS_RMS = 1e-06
EPS_LN = 1e-05

def block_count(length):
    number = max(1, length // 512)
    while length % number:
        number = number - 1
    return number

def attend_block(query_rows, key_heads, value_heads, query_segs, key_segs):
    scores = jnp.einsum('hqd,hkd->hqk', query_rows.astype(jnp.float32), key_heads.astype(jnp.float32)) * HD ** (-0.5)
    same_image = query_segs[:, None] == key_segs[None, :]
    scores = jnp.where(same_image[None], scores, -jnp.inf)
    row_max = lax.optimization_barrier(jnp.max(scores, axis=-1, keepdims=True))
    weights = jnp.exp(scores - row_max)
    probabilities = (weights / lax.optimization_barrier(jnp.sum(weights, axis=-1, keepdims=True))).astype(jnp.bfloat16)
    mixed = jnp.einsum('hqk,hkd->hqd', probabilities.astype(jnp.float32), value_heads.astype(jnp.float32))
    return mixed.astype(jnp.bfloat16)

def merge_rows(stream):
    feature_count = stream.shape[-1]
    shaped = stream.reshape(stream.shape[0] // (2 * PW), 2, PW // 2, 2, feature_count)
    return shaped.transpose(0, 2, 1, 3, 4).reshape(stream.shape[0] // 4, 4, feature_count)

def reference(tokens, segments, norm_gain, wqkv, qk_gain, wproj, bproj, layer_scale, ln_weight, ln_bias, w_merge, b_merge, owners):
    inner_width = HEADS * HD

    def encode_group(group_item):
        group_tokens, group_segs = group_item
        widened = group_tokens.astype(jnp.float32)
        normed = (widened * lax.rsqrt(lax.optimization_barrier(jnp.mean(widened * widened, axis=-1, keepdims=True)) + EPS_RMS) * norm_gain).astype(jnp.bfloat16)
        q_part = jnp.dot(normed, wqkv[0], preferred_element_type=jnp.float32)
        k_part = jnp.dot(normed, wqkv[1], preferred_element_type=jnp.float32)
        v_part = jnp.dot(normed, wqkv[2], preferred_element_type=jnp.float32)
        q_scaled = (q_part * lax.rsqrt(lax.optimization_barrier(jnp.mean(q_part * q_part, axis=-1, keepdims=True)) + EPS_RMS) * qk_gain[0]).astype(jnp.bfloat16)
        k_scaled = (k_part * lax.rsqrt(lax.optimization_barrier(jnp.mean(k_part * k_part, axis=-1, keepdims=True)) + EPS_RMS) * qk_gain[1]).astype(jnp.bfloat16)
        v_scaled = v_part.astype(jnp.bfloat16)

        def split_heads(matrix):
            return matrix.reshape(TOK, HEADS, HD).transpose(1, 0, 2)
        block_total = block_count(TOK)
        block_rows = TOK // block_total
        query_blocks = split_heads(q_scaled).reshape(HEADS, block_total, block_rows, HD).transpose(1, 0, 2, 3)
        seg_blocks = group_segs.reshape(block_total, block_rows)
        key_heads = split_heads(k_scaled)
        value_heads = split_heads(v_scaled)
        mixed = lax.map(lambda block_item: attend_block(block_item[0], key_heads, value_heads, block_item[1], group_segs), (query_blocks, seg_blocks))
        attended = mixed.transpose(0, 2, 1, 3).reshape(TOK, inner_width)
        attn_out = jnp.dot(attended, wproj, preferred_element_type=jnp.float32)
        stream = (widened + layer_scale * (attn_out + bproj)).astype(jnp.bfloat16)
        merged = merge_rows(stream).reshape(MERGED, 4 * D).astype(jnp.float32)
        row_mean = lax.optimization_barrier(jnp.mean(merged, axis=-1, keepdims=True))
        centered = merged - row_mean
        row_var = lax.optimization_barrier(jnp.mean(centered * centered, axis=-1, keepdims=True))
        normal_rows = (centered * lax.rsqrt(row_var + EPS_LN) * ln_weight.reshape(4 * D) + ln_bias.reshape(4 * D)).astype(jnp.bfloat16)
        lifted = jnp.dot(normal_rows, w_merge.reshape(4 * D, PF), preferred_element_type=jnp.float32) + b_merge
        first_tokens = merge_rows(group_segs.reshape(TOK, 1))[:, 0, 0]
        live_rows = (first_tokens >= 0).astype(jnp.float32)
        return (jax.nn.gelu(lifted, approximate=False) * live_rows[:, None]).astype(jnp.bfloat16)
    projected = lax.map(encode_group, (tokens, segments))
    owner_ids = owners[:, :, 0].reshape(N_REQ, N_TP, MD)
    group_ids = jnp.arange(N_REQ, dtype=jnp.int32)
    owner_hits = (owner_ids[..., None] == group_ids).astype(jnp.int32)
    before = jnp.cumsum(owner_hits, axis=2) - owner_hits
    slot_rank = lax.optimization_barrier(jnp.sum(before * owner_hits, axis=-1))
    slot_ids = jnp.arange(CAP, dtype=jnp.int32)
    selector = (owner_ids[None, :, :, None, :] == group_ids[:, None, None, None, None]) & (slot_rank[None, :, :, None, :] == slot_ids[None, None, None, :, None])
    lm_inputs = jnp.einsum('dstcm,stmf->dstcf', selector.astype(jnp.float32), projected.reshape(N_REQ, N_TP, MD, PF).astype(jnp.float32))
    return lm_inputs.astype(jnp.bfloat16)
```

```python
import jax
import jax.numpy as jnp
from jax import lax
from jax.sharding import Mesh
from jax.sharding import PartitionSpec as P

D = 3200
HEADS = 16
HD = 128
PW = 32


EPS_RMS = 1e-06
EPS_LN = 1e-05

TP_AXES = ("ty", "tz")


def block_count(length):
    number = max(1, length // 512)
    while length % number:
        number = number - 1
    return number


def attend_block(query_rows, key_heads, value_heads, query_segs, key_segs):
    scores = jnp.einsum(
        "hqd,hkd->hqk", query_rows, key_heads, preferred_element_type=jnp.float32
    ) * HD ** (-0.5)
    same_image = query_segs[:, None] == key_segs[None, :]
    scores = jnp.where(same_image[None], scores, -jnp.inf)
    row_max = jnp.max(scores, axis=-1, keepdims=True)
    weights = jnp.exp(scores - row_max)
    probabilities = (weights / jnp.sum(weights, axis=-1, keepdims=True)).astype(jnp.bfloat16)
    mixed = jnp.einsum(
        "hqk,hkd->hqd", probabilities, value_heads, preferred_element_type=jnp.float32
    )
    return mixed.astype(jnp.bfloat16)


def merge_rows(stream):
    feature_count = stream.shape[-1]
    shaped = stream.reshape(stream.shape[0] // (2 * PW), 2, PW // 2, 2, feature_count)
    return shaped.transpose(0, 2, 1, 3, 4).reshape(stream.shape[0] // 4, 4, feature_count)


def slot_ranks(owner_ids, group_total):
    owner_hits = (owner_ids[:, None] == jnp.arange(group_total, dtype=jnp.int32)[None, :]).astype(
        jnp.int32
    )
    before = jnp.cumsum(owner_hits, axis=0) - owner_hits
    return jnp.sum(before * owner_hits, axis=1)


def tp_gather(value, axis):
    inner = lax.all_gather(value, "tz", axis=axis, tiled=True)
    return lax.all_gather(inner, "ty", axis=axis, tiled=True)


def tp_scatter_sum(value, axis):
    outer = lax.psum_scatter(value, "ty", scatter_dimension=axis, tiled=True)
    return lax.psum_scatter(outer, "tz", scatter_dimension=axis, tiled=True)


def per_device(
    tokens,
    segments,
    norm_gain,
    wqkv,
    qk_gain,
    wproj,
    bproj,
    layer_scale,
    ln_weight,
    ln_bias,
    w_merge,
    b_merge,
    owners,
):
    tp_total = lax.axis_size("ty") * lax.axis_size("tz")
    tp_index = lax.axis_index("ty") * lax.axis_size("tz") + lax.axis_index("tz")
    req_index = lax.axis_index("req")
    group_total = lax.axis_size("req")
    gathered = tp_gather(tokens, 1)[0]
    seq_len = gathered.shape[0]
    group_segs = segments[0]
    widened = gathered.astype(jnp.float32)
    normed = (
        widened
        * lax.rsqrt(jnp.mean(widened * widened, axis=-1, keepdims=True) + EPS_RMS)
        * norm_gain
    ).astype(jnp.bfloat16)
    proj_qkv = jnp.einsum("td,ide->ite", normed, wqkv, preferred_element_type=jnp.float32)
    q_part = proj_qkv[0]
    k_part = proj_qkv[1]
    v_part = proj_qkv[2]
    square_sums = lax.psum(
        (jnp.sum(q_part * q_part, axis=-1), jnp.sum(k_part * k_part, axis=-1)), TP_AXES
    )
    inner_width = HEADS * HD
    q_scaled = (
        q_part * lax.rsqrt(square_sums[0] / inner_width + EPS_RMS)[:, None] * qk_gain[0]
    ).astype(jnp.bfloat16)
    k_scaled = (
        k_part * lax.rsqrt(square_sums[1] / inner_width + EPS_RMS)[:, None] * qk_gain[1]
    ).astype(jnp.bfloat16)
    v_scaled = v_part.astype(jnp.bfloat16)
    heads_here = q_part.shape[1] // HD

    def split_heads(matrix):
        return matrix.reshape(seq_len, heads_here, HD).transpose(1, 0, 2)

    block_total = block_count(seq_len)
    block_rows = seq_len // block_total
    query_blocks = (
        split_heads(q_scaled).reshape(heads_here, block_total, block_rows, HD).transpose(1, 0, 2, 3)
    )
    seg_blocks = group_segs.reshape(block_total, block_rows)
    key_heads = split_heads(k_scaled)
    value_heads = split_heads(v_scaled)
    mixed = lax.map(
        lambda block_item: attend_block(
            block_item[0], key_heads, value_heads, block_item[1], group_segs
        ),
        (query_blocks, seg_blocks),
    )
    attended = mixed.transpose(0, 2, 1, 3).reshape(seq_len, heads_here * HD)
    width_dev = bproj.shape[0]
    head_part = jnp.dot(attended, wproj, preferred_element_type=jnp.float32)
    attn_out = tp_scatter_sum(head_part.astype(jnp.bfloat16), 1).astype(jnp.float32)
    own_columns = lax.dynamic_slice_in_dim(gathered, tp_index * width_dev, width_dev, 1).astype(
        jnp.float32
    )
    stream = (own_columns + layer_scale * (attn_out + bproj)).astype(jnp.bfloat16)
    merged = merge_rows(stream).astype(jnp.float32)
    feature_total = 4 * D
    local_count = 4 * width_dev
    local_sum = jnp.sum(merged, axis=(1, 2))
    local_mean = local_sum / local_count
    local_dev = merged - local_mean[:, None, None]
    local_m2 = jnp.sum(local_dev * local_dev, axis=(1, 2))
    stats = lax.all_gather(jnp.stack([local_sum, local_m2]), TP_AXES, axis=0, tiled=False)
    row_mean = jnp.sum(stats[:, 0], axis=0) / feature_total
    spread = stats[:, 0] / local_count - row_mean[None, :]
    row_m2 = jnp.sum(stats[:, 1], axis=0) + local_count * jnp.sum(spread * spread, axis=0)
    row_var = row_m2 / feature_total
    centered = merged - row_mean[:, None, None]
    normal_rows = (
        centered * lax.rsqrt(row_var + EPS_LN)[:, None, None] * ln_weight + ln_bias
    ).astype(jnp.bfloat16)
    merged_total = normal_rows.shape[0]
    flat_rows = normal_rows.reshape(merged_total, 4 * width_dev)
    flat_weight = w_merge.reshape(4 * width_dev, w_merge.shape[2])
    merged_dev = merged_total // tp_total
    own_rows = tp_scatter_sum(
        jnp.dot(flat_rows, flat_weight, preferred_element_type=jnp.float32).astype(jnp.bfloat16),
        0,
    ).astype(jnp.float32)
    first_tokens = merge_rows(group_segs.reshape(seq_len, 1))[:, 0, 0]
    own_first = lax.dynamic_slice_in_dim(first_tokens, tp_index * merged_dev, merged_dev, 0)
    live_rows = (own_first >= 0).astype(jnp.float32)
    out_rows = (jax.nn.gelu(own_rows + b_merge, approximate=False) * live_rows[:, None]).astype(
        jnp.bfloat16
    )
    capacity = (merged_dev + group_total - 1) // group_total + 1
    group_ids = jnp.arange(group_total, dtype=jnp.int32)
    slot_ids = jnp.arange(capacity, dtype=jnp.int32)
    mine_ids = lax.dynamic_index_in_dim(owners[:, :, 0], req_index, 0, keepdims=False)
    slot_rank = slot_ranks(mine_ids, group_total)
    selector = (mine_ids[None, None, :] == group_ids[:, None, None]) & (
        slot_rank[None, None, :] == slot_ids[None, :, None]
    )
    outgoing = jnp.einsum(
        "gcm,mf->gcf", selector.astype(jnp.bfloat16), out_rows, preferred_element_type=jnp.float32
    ).astype(jnp.bfloat16)
    incoming = lax.all_to_all(outgoing, "req", split_axis=0, concat_axis=0, tiled=True)
    return incoming.reshape(1, group_total, 1, capacity, incoming.shape[-1])


def solution(mesh):
    grid = mesh.devices
    inner = 4 if grid.shape[1] % 4 == 0 else 1
    split = Mesh(
        grid.reshape(grid.shape[0], grid.shape[1] // inner, inner), ("req",) + TP_AXES
    )
    tp = TP_AXES
    placed = (
        P("req", tp, None),
        P("req", None),
        P(),
        P(None, None, tp),
        P(None, tp),
        P(tp, None),
        P(tp),
        P(tp),
        P(None, tp),
        P(None, tp),
        P(None, tp, None),
        P(),
        P(None, tp, None),
    )
    return jax.shard_map(
        per_device,
        mesh=split,
        in_specs=placed,
        out_specs=P("req", None, tp, None, None),
        check_vma=False,
    )
```

```python
import jax
import jax.numpy as jnp
from jax import lax
from jax.sharding import Mesh
from jax.sharding import PartitionSpec as P

D = 3200
HEADS = 16
HD = 128
PW = 32


EPS_RMS = 1e-06
EPS_LN = 1e-05

TP_AXES = ("ty", "tz")


def block_count(length):
    number = max(1, length // 512)
    while length % number:
        number = number - 1
    return number


def attend_block(query_rows, key_heads, value_heads, query_segs, key_segs):
    scores = jnp.einsum(
        "hqd,hkd->hqk", query_rows, key_heads, preferred_element_type=jnp.float32
    ) * HD ** (-0.5)
    same_image = query_segs[:, None] == key_segs[None, :]
    scores = jnp.where(same_image[None], scores, -jnp.inf)
    row_max = jnp.max(scores, axis=-1, keepdims=True)
    weights = jnp.exp(scores - row_max)
    probabilities = (weights / jnp.sum(weights, axis=-1, keepdims=True)).astype(jnp.bfloat16)
    mixed = jnp.einsum(
        "hqk,hkd->hqd", probabilities, value_heads, preferred_element_type=jnp.float32
    )
    return mixed.astype(jnp.bfloat16)


def merge_rows(stream):
    feature_count = stream.shape[-1]
    shaped = stream.reshape(stream.shape[0] // (2 * PW), 2, PW // 2, 2, feature_count)
    return shaped.transpose(0, 2, 1, 3, 4).reshape(stream.shape[0] // 4, 4, feature_count)


def slot_ranks(owner_ids, group_total):
    owner_hits = (owner_ids[:, None] == jnp.arange(group_total, dtype=jnp.int32)[None, :]).astype(
        jnp.int32
    )
    before = jnp.cumsum(owner_hits, axis=0) - owner_hits
    return jnp.sum(before * owner_hits, axis=1)


def tp_gather(value, axis):
    inner = lax.all_gather(value, "tz", axis=axis, tiled=True)
    return lax.all_gather(inner, "ty", axis=axis, tiled=True)


def tp_scatter_sum(value, axis):
    outer = lax.psum_scatter(value, "ty", scatter_dimension=axis, tiled=True)
    return lax.psum_scatter(outer, "tz", scatter_dimension=axis, tiled=True)


def scatter_sum_exchange(value, axis_name, axis):
    count = lax.axis_size(axis_name)
    shape = value.shape
    parts = value.reshape(shape[:axis] + (count, shape[axis] // count) + shape[axis + 1 :])
    got = lax.all_to_all(parts, axis_name, split_axis=axis, concat_axis=axis, tiled=True)
    return jnp.sum(got.astype(jnp.float32), axis=axis)


def butterfly_gather(value):
    out = value
    for axis_name in ("tz", "ty"):
        count = lax.axis_size(axis_name)
        step = 1
        while step < count:
            swap = [(i, i ^ step) for i in range(count)]
            out = jnp.concatenate([out, lax.ppermute(out, axis_name, swap)], axis=0)
            step = step * 2
    return out


def per_device(
    tokens,
    segments,
    norm_gain,
    wqkv,
    qk_gain,
    wproj,
    bproj,
    layer_scale,
    ln_weight,
    ln_bias,
    w_merge,
    b_merge,
    owners,
):
    tp_total = lax.axis_size("ty") * lax.axis_size("tz")
    tp_index = lax.axis_index("ty") * lax.axis_size("tz") + lax.axis_index("tz")
    req_index = lax.axis_index("req")
    group_total = lax.axis_size("req")
    gathered = tp_gather(tokens, 1)[0]
    seq_len = gathered.shape[0]
    group_segs = segments[0]
    widened = gathered.astype(jnp.float32)
    normed = (
        widened
        * lax.rsqrt(jnp.mean(widened * widened, axis=-1, keepdims=True) + EPS_RMS)
        * norm_gain
    ).astype(jnp.bfloat16)
    proj_qkv = jnp.einsum("td,ide->ite", normed, wqkv, preferred_element_type=jnp.float32)
    q_part = proj_qkv[0]
    k_part = proj_qkv[1]
    v_part = proj_qkv[2]
    square_sums = lax.psum(
        lax.psum(jnp.stack([jnp.sum(q_part * q_part, axis=-1), jnp.sum(k_part * k_part, axis=-1)]), "tz"),
        "ty",
    )
    inner_width = HEADS * HD
    q_scaled = (
        q_part * lax.rsqrt(square_sums[0] / inner_width + EPS_RMS)[:, None] * qk_gain[0]
    ).astype(jnp.bfloat16)
    k_scaled = (
        k_part * lax.rsqrt(square_sums[1] / inner_width + EPS_RMS)[:, None] * qk_gain[1]
    ).astype(jnp.bfloat16)
    v_scaled = v_part.astype(jnp.bfloat16)
    heads_here = q_part.shape[1] // HD

    def split_heads(matrix):
        return matrix.reshape(seq_len, heads_here, HD).transpose(1, 0, 2)

    block_total = block_count(seq_len)
    block_rows = seq_len // block_total
    query_blocks = (
        split_heads(q_scaled).reshape(heads_here, block_total, block_rows, HD).transpose(1, 0, 2, 3)
    )
    seg_blocks = group_segs.reshape(block_total, block_rows)
    key_heads = split_heads(k_scaled)
    value_heads = split_heads(v_scaled)
    mixed = lax.map(
        lambda block_item: attend_block(
            block_item[0], key_heads, value_heads, block_item[1], group_segs
        ),
        (query_blocks, seg_blocks),
    )
    attended = mixed.transpose(0, 2, 1, 3).reshape(seq_len, heads_here * HD)
    width_dev = bproj.shape[0]
    head_part = jnp.dot(attended, wproj, preferred_element_type=jnp.float32)
    attn_outer = lax.psum_scatter(head_part.astype(jnp.bfloat16), "ty", scatter_dimension=1, tiled=True)
    attn_out = scatter_sum_exchange(attn_outer, "tz", 1)
    own_columns = lax.dynamic_slice_in_dim(gathered, tp_index * width_dev, width_dev, 1).astype(
        jnp.float32
    )
    stream = (own_columns + layer_scale * (attn_out + bproj)).astype(jnp.bfloat16)
    merged = merge_rows(stream).astype(jnp.float32)
    feature_total = 4 * D
    local_count = 4 * width_dev
    local_sum = jnp.sum(merged, axis=(1, 2))
    local_mean = local_sum / local_count
    local_dev = merged - local_mean[:, None, None]
    local_m2 = jnp.sum(local_dev * local_dev, axis=(1, 2))
    stats = butterfly_gather(jnp.stack([local_sum, local_m2])[None])
    row_mean = jnp.sum(stats[:, 0], axis=0) / feature_total
    spread = stats[:, 0] / local_count - row_mean[None, :]
    row_m2 = jnp.sum(stats[:, 1], axis=0) + local_count * jnp.sum(spread * spread, axis=0)
    row_var = row_m2 / feature_total
    centered = merged - row_mean[:, None, None]
    normal_rows = (
        centered * lax.rsqrt(row_var + EPS_LN)[:, None, None] * ln_weight + ln_bias
    ).astype(jnp.bfloat16)
    merged_total = normal_rows.shape[0]
    flat_rows = normal_rows.reshape(merged_total, 4 * width_dev)
    flat_weight = w_merge.reshape(4 * width_dev, w_merge.shape[2])
    merged_dev = merged_total // tp_total
    own_rows = tp_scatter_sum(
        jnp.dot(flat_rows, flat_weight, preferred_element_type=jnp.float32).astype(jnp.bfloat16),
        0,
    ).astype(jnp.float32)
    first_tokens = merge_rows(group_segs.reshape(seq_len, 1))[:, 0, 0]
    own_first = lax.dynamic_slice_in_dim(first_tokens, tp_index * merged_dev, merged_dev, 0)
    live_rows = (own_first >= 0).astype(jnp.float32)
    out_rows = (jax.nn.gelu(own_rows + b_merge, approximate=False) * live_rows[:, None]).astype(
        jnp.bfloat16
    )
    capacity = (merged_dev + group_total - 1) // group_total + 1
    group_ids = jnp.arange(group_total, dtype=jnp.int32)
    slot_ids = jnp.arange(capacity, dtype=jnp.int32)
    mine_ids = lax.dynamic_index_in_dim(owners[:, :, 0], req_index, 0, keepdims=False)
    slot_rank = slot_ranks(mine_ids, group_total)
    selector = (mine_ids[None, None, :] == group_ids[:, None, None]) & (
        slot_rank[None, None, :] == slot_ids[None, :, None]
    )
    outgoing = jnp.einsum(
        "gcm,mf->gcf", selector.astype(jnp.bfloat16), out_rows, preferred_element_type=jnp.float32
    ).astype(jnp.bfloat16)
    incoming = lax.all_to_all(outgoing, "req", split_axis=0, concat_axis=0, tiled=True)
    return incoming.reshape(1, group_total, 1, capacity, incoming.shape[-1])


def solution(mesh):
    grid = mesh.devices
    inner = 4 if grid.shape[1] % 4 == 0 else 1
    split = Mesh(
        grid.reshape(grid.shape[0], grid.shape[1] // inner, inner), ("req",) + TP_AXES
    )
    tp = TP_AXES
    placed = (
        P("req", tp, None),
        P("req", None),
        P(),
        P(None, None, tp),
        P(None, tp),
        P(tp, None),
        P(tp),
        P(tp),
        P(None, tp),
        P(None, tp),
        P(None, tp, None),
        P(),
        P(None, tp, None),
    )
    return jax.shard_map(
        per_device,
        mesh=split,
        in_specs=placed,
        out_specs=P("req", None, tp, None, None),
        check_vma=False,
    )
```

```python
import jax
import jax.numpy as jnp
from jax import lax
from jax.sharding import Mesh
from jax.sharding import PartitionSpec as P

D = 3200
HEADS = 16
HD = 128
PW = 32


EPS_RMS = 1e-06
EPS_LN = 1e-05

TP_AXES = ("ty", "tz")


def block_count(length):
    number = max(1, length // 512)
    while length % number:
        number = number - 1
    return number


def attend_block(query_rows, key_heads, value_heads, query_segs, key_segs):
    scores = jnp.einsum(
        "hqd,hkd->hqk", query_rows, key_heads, preferred_element_type=jnp.float32
    ) * HD ** (-0.5)
    same_image = query_segs[:, None] == key_segs[None, :]
    scores = jnp.where(same_image[None], scores, -jnp.inf)
    row_max = jnp.max(scores, axis=-1, keepdims=True)
    weights = jnp.exp(scores - row_max)
    probabilities = (weights / jnp.sum(weights, axis=-1, keepdims=True)).astype(jnp.bfloat16)
    mixed = jnp.einsum(
        "hqk,hkd->hqd", probabilities, value_heads, preferred_element_type=jnp.float32
    )
    return mixed.astype(jnp.bfloat16)


def merge_rows(stream):
    feature_count = stream.shape[-1]
    shaped = stream.reshape(stream.shape[0] // (2 * PW), 2, PW // 2, 2, feature_count)
    return shaped.transpose(0, 2, 1, 3, 4).reshape(stream.shape[0] // 4, 4, feature_count)


def slot_ranks(owner_ids, group_total):
    owner_hits = (owner_ids[:, None] == jnp.arange(group_total, dtype=jnp.int32)[None, :]).astype(
        jnp.int32
    )
    before = jnp.cumsum(owner_hits, axis=0) - owner_hits
    return jnp.sum(before * owner_hits, axis=1)


def axis_exchange(value, axis_name):
    count = lax.axis_size(axis_name)
    got = [value]
    for shift in range(1, count):
        ring = [(i, (i + shift) % count) for i in range(count)]
        got.append(lax.ppermute(value, axis_name, ring))
    return got


def tp_gather(value, axis):
    count = lax.axis_size("tz")
    got = axis_exchange(value, "tz")
    ordered = jnp.stack([got[(count - k) % count] for k in range(count)], axis=0)
    ordered = jnp.roll(ordered, lax.axis_index("tz"), axis=0)
    inner = jnp.concatenate([ordered[k] for k in range(count)], axis=axis)
    return lax.all_gather(inner, "ty", axis=axis, tiled=True)


def exchange_sum(value):
    for axis_name in ("tz", "ty"):
        got = axis_exchange(value, axis_name)
        value = sum(got[1:], got[0])
    return value


def exchange_gather(value):
    for axis_name in ("tz", "ty"):
        value = jnp.concatenate(axis_exchange(value, axis_name), axis=0)
    return value


def tp_scatter_sum(value, axis):
    outer = lax.psum_scatter(value, "ty", scatter_dimension=axis, tiled=True)
    return lax.psum_scatter(outer, "tz", scatter_dimension=axis, tiled=True)


def scatter_sum_exchange(value, axis_name, axis):
    count = lax.axis_size(axis_name)
    shape = value.shape
    parts = value.reshape(shape[:axis] + (count, shape[axis] // count) + shape[axis + 1 :])
    got = lax.all_to_all(parts, axis_name, split_axis=axis, concat_axis=axis, tiled=True)
    return jnp.sum(got.astype(jnp.float32), axis=axis)


def butterfly_gather(value):
    out = value
    for axis_name in ("tz", "ty"):
        count = lax.axis_size(axis_name)
        step = 1
        while step < count:
            swap = [(i, i ^ step) for i in range(count)]
            out = jnp.concatenate([out, lax.ppermute(out, axis_name, swap)], axis=0)
            step = step * 2
    return out


def per_device(
    tokens,
    segments,
    norm_gain,
    wqkv,
    qk_gain,
    wproj,
    bproj,
    layer_scale,
    ln_weight,
    ln_bias,
    w_merge,
    b_merge,
    owners,
):
    tp_total = lax.axis_size("ty") * lax.axis_size("tz")
    tp_index = lax.axis_index("ty") * lax.axis_size("tz") + lax.axis_index("tz")
    req_index = lax.axis_index("req")
    group_total = lax.axis_size("req")
    gathered = tp_gather(tokens, 1)[0]
    seq_len = gathered.shape[0]
    group_segs = segments[0]
    widened = gathered.astype(jnp.float32)
    normed = (
        widened
        * lax.rsqrt(jnp.mean(widened * widened, axis=-1, keepdims=True) + EPS_RMS)
        * norm_gain
    ).astype(jnp.bfloat16)
    proj_qkv = jnp.einsum("td,ide->ite", normed, wqkv, preferred_element_type=jnp.float32)
    q_part = proj_qkv[0]
    k_part = proj_qkv[1]
    v_part = proj_qkv[2]
    square_sums = exchange_sum(
        jnp.stack([jnp.sum(q_part * q_part, axis=-1), jnp.sum(k_part * k_part, axis=-1)])
    )
    inner_width = HEADS * HD
    q_scaled = (
        q_part * lax.rsqrt(square_sums[0] / inner_width + EPS_RMS)[:, None] * qk_gain[0]
    ).astype(jnp.bfloat16)
    k_scaled = (
        k_part * lax.rsqrt(square_sums[1] / inner_width + EPS_RMS)[:, None] * qk_gain[1]
    ).astype(jnp.bfloat16)
    v_scaled = v_part.astype(jnp.bfloat16)
    heads_here = q_part.shape[1] // HD

    def split_heads(matrix):
        return matrix.reshape(seq_len, heads_here, HD).transpose(1, 0, 2)

    block_total = block_count(seq_len)
    block_rows = seq_len // block_total
    query_blocks = (
        split_heads(q_scaled).reshape(heads_here, block_total, block_rows, HD).transpose(1, 0, 2, 3)
    )
    seg_blocks = group_segs.reshape(block_total, block_rows)
    key_heads = split_heads(k_scaled)
    value_heads = split_heads(v_scaled)
    mixed = lax.map(
        lambda block_item: attend_block(
            block_item[0], key_heads, value_heads, block_item[1], group_segs
        ),
        (query_blocks, seg_blocks),
    )
    attended = mixed.transpose(0, 2, 1, 3).reshape(seq_len, heads_here * HD)
    width_dev = bproj.shape[0]
    head_part = jnp.dot(attended, wproj, preferred_element_type=jnp.float32)
    attn_outer = lax.psum_scatter(head_part.astype(jnp.bfloat16), "ty", scatter_dimension=1, tiled=True)
    attn_out = scatter_sum_exchange(attn_outer, "tz", 1)
    own_columns = lax.dynamic_slice_in_dim(gathered, tp_index * width_dev, width_dev, 1).astype(
        jnp.float32
    )
    stream = (own_columns + layer_scale * (attn_out + bproj)).astype(jnp.bfloat16)
    merged = merge_rows(stream).astype(jnp.float32)
    feature_total = 4 * D
    local_count = 4 * width_dev
    local_sum = jnp.sum(merged, axis=(1, 2))
    local_mean = local_sum / local_count
    local_dev = merged - local_mean[:, None, None]
    local_m2 = jnp.sum(local_dev * local_dev, axis=(1, 2))
    stats = exchange_gather(jnp.stack([local_sum, local_m2])[None])
    row_mean = jnp.sum(stats[:, 0], axis=0) / feature_total
    spread = stats[:, 0] / local_count - row_mean[None, :]
    row_m2 = jnp.sum(stats[:, 1], axis=0) + local_count * jnp.sum(spread * spread, axis=0)
    row_var = row_m2 / feature_total
    centered = merged - row_mean[:, None, None]
    normal_rows = (
        centered * lax.rsqrt(row_var + EPS_LN)[:, None, None] * ln_weight + ln_bias
    ).astype(jnp.bfloat16)
    merged_total = normal_rows.shape[0]
    flat_rows = normal_rows.reshape(merged_total, 4 * width_dev)
    flat_weight = w_merge.reshape(4 * width_dev, w_merge.shape[2])
    merged_dev = merged_total // tp_total
    row_part = jnp.dot(flat_rows, flat_weight, preferred_element_type=jnp.float32)
    row_outer = lax.psum_scatter(row_part.astype(jnp.bfloat16), "ty", scatter_dimension=0, tiled=True)
    own_rows = scatter_sum_exchange(row_outer, "tz", 0)
    first_tokens = merge_rows(group_segs.reshape(seq_len, 1))[:, 0, 0]
    own_first = lax.dynamic_slice_in_dim(first_tokens, tp_index * merged_dev, merged_dev, 0)
    live_rows = (own_first >= 0).astype(jnp.float32)
    out_rows = (jax.nn.gelu(own_rows + b_merge, approximate=False) * live_rows[:, None]).astype(
        jnp.bfloat16
    )
    capacity = (merged_dev + group_total - 1) // group_total + 1
    group_ids = jnp.arange(group_total, dtype=jnp.int32)
    slot_ids = jnp.arange(capacity, dtype=jnp.int32)
    mine_ids = lax.dynamic_index_in_dim(owners[:, :, 0], req_index, 0, keepdims=False)
    slot_rank = slot_ranks(mine_ids, group_total)
    selector = (mine_ids[None, None, :] == group_ids[:, None, None]) & (
        slot_rank[None, None, :] == slot_ids[None, :, None]
    )
    outgoing = jnp.einsum(
        "gcm,mf->gcf", selector.astype(jnp.bfloat16), out_rows, preferred_element_type=jnp.float32
    ).astype(jnp.bfloat16)
    incoming = lax.all_to_all(outgoing, "req", split_axis=0, concat_axis=0, tiled=True)
    return incoming.reshape(1, group_total, 1, capacity, incoming.shape[-1])


def solution(mesh):
    grid = mesh.devices
    inner = 4 if grid.shape[1] % 4 == 0 else 1
    split = Mesh(
        grid.reshape(grid.shape[0], grid.shape[1] // inner, inner), ("req",) + TP_AXES
    )
    tp = TP_AXES
    placed = (
        P("req", tp, None),
        P("req", None),
        P(),
        P(None, None, tp),
        P(None, tp),
        P(tp, None),
        P(tp),
        P(tp),
        P(None, tp),
        P(None, tp),
        P(None, tp, None),
        P(),
        P(None, tp, None),
    )
    return jax.shard_map(
        per_device,
        mesh=split,
        in_specs=placed,
        out_specs=P("req", None, tp, None, None),
        check_vma=False,
    )
```

```python
import jax
import jax.numpy as jnp
from jax import lax
from jax.sharding import Mesh
from jax.sharding import PartitionSpec as P

D = 3200
HEADS = 16
HD = 128
PW = 32


EPS_RMS = 1e-06
EPS_LN = 1e-05

TP_AXES = ("ty", "tz")


def block_count(length):
    number = max(1, length // 512)
    while length % number:
        number = number - 1
    return number


def attend_block(query_rows, key_heads, value_heads, query_segs, key_segs):
    scores = jnp.einsum(
        "hqd,hkd->hqk", query_rows, key_heads, preferred_element_type=jnp.float32
    ) * HD ** (-0.5)
    same_image = query_segs[:, None] == key_segs[None, :]
    scores = jnp.where(same_image[None], scores, -jnp.inf)
    row_max = jnp.max(scores, axis=-1, keepdims=True)
    weights = jnp.exp(scores - row_max)
    probabilities = (weights / jnp.sum(weights, axis=-1, keepdims=True)).astype(jnp.bfloat16)
    mixed = jnp.einsum(
        "hqk,hkd->hqd", probabilities, value_heads, preferred_element_type=jnp.float32
    )
    return mixed.astype(jnp.bfloat16)


def merge_rows(stream):
    feature_count = stream.shape[-1]
    shaped = stream.reshape(stream.shape[0] // (2 * PW), 2, PW // 2, 2, feature_count)
    return shaped.transpose(0, 2, 1, 3, 4).reshape(stream.shape[0] // 4, 4, feature_count)


def slot_ranks(owner_ids, group_total):
    owner_hits = (owner_ids[:, None] == jnp.arange(group_total, dtype=jnp.int32)[None, :]).astype(
        jnp.int32
    )
    before = jnp.cumsum(owner_hits, axis=0) - owner_hits
    return jnp.sum(before * owner_hits, axis=1)


def axis_exchange(value, axis_name):
    count = lax.axis_size(axis_name)
    got = [value]
    for shift in range(1, count):
        ring = [(i, (i + shift) % count) for i in range(count)]
        got.append(lax.ppermute(value, axis_name, ring))
    return got


def tp_gather(value, axis):
    count = lax.axis_size("tz")
    got = axis_exchange(value, "tz")
    ordered = jnp.stack([got[(count - k) % count] for k in range(count)], axis=0)
    ordered = jnp.roll(ordered, lax.axis_index("tz"), axis=0)
    inner = jnp.concatenate([ordered[k] for k in range(count)], axis=axis)
    return lax.all_gather(inner, "ty", axis=axis, tiled=True)


def exchange_sum(value):
    for axis_name in ("tz", "ty"):
        got = axis_exchange(value, axis_name)
        value = sum(got[1:], got[0])
    return value


def exchange_gather(value):
    for axis_name in ("tz", "ty"):
        value = jnp.concatenate(axis_exchange(value, axis_name), axis=0)
    return value


def tp_scatter_sum(value, axis):
    outer = lax.psum_scatter(value, "ty", scatter_dimension=axis, tiled=True)
    return lax.psum_scatter(outer, "tz", scatter_dimension=axis, tiled=True)


def scatter_sum_exchange(value, axis_name, axis):
    count = lax.axis_size(axis_name)
    shape = value.shape
    parts = value.reshape(shape[:axis] + (count, shape[axis] // count) + shape[axis + 1 :])
    got = lax.all_to_all(parts, axis_name, split_axis=axis, concat_axis=axis, tiled=True)
    return jnp.sum(got.astype(jnp.float32), axis=axis)


def butterfly_gather(value):
    out = value
    for axis_name in ("tz", "ty"):
        count = lax.axis_size(axis_name)
        step = 1
        while step < count:
            swap = [(i, i ^ step) for i in range(count)]
            out = jnp.concatenate([out, lax.ppermute(out, axis_name, swap)], axis=0)
            step = step * 2
    return out


def column_shards(weight):
    ty_count = lax.axis_size("ty")
    tz_count = lax.axis_size("tz")
    rows, cols = weight.shape
    width = cols // (ty_count * tz_count)
    parts = weight.reshape(1, 1, rows, ty_count, tz_count, width)
    parts = lax.all_to_all(parts, "tz", split_axis=4, concat_axis=1, tiled=True)
    parts = lax.all_to_all(parts, "ty", split_axis=3, concat_axis=0, tiled=True)
    return parts.reshape(ty_count * tz_count * rows, width)


def req_exchange(outgoing):
    count = lax.axis_size("req")
    mine = lax.axis_index("req")
    ahead = jnp.roll(outgoing, -mine, axis=0)
    got = [ahead[0]]
    for shift in range(1, count):
        ring = [(i, (i + shift) % count) for i in range(count)]
        got.append(lax.ppermute(ahead[shift], "req", ring))
    ordered = jnp.stack([got[(count - k) % count] for k in range(count)], axis=0)
    return jnp.roll(ordered, mine, axis=0)


def per_device(
    tokens,
    segments,
    norm_gain,
    wqkv,
    qk_gain,
    wproj,
    bproj,
    layer_scale,
    ln_weight,
    ln_bias,
    w_merge,
    b_merge,
    owners,
):
    tp_total = lax.axis_size("ty") * lax.axis_size("tz")
    tp_index = lax.axis_index("ty") * lax.axis_size("tz") + lax.axis_index("tz")
    req_index = lax.axis_index("req")
    group_total = lax.axis_size("req")
    gathered, wproj_cols = lax.optimization_barrier((tp_gather(tokens, 1)[0], column_shards(wproj)))
    seq_len = gathered.shape[0]
    group_segs = segments[0]
    widened = gathered.astype(jnp.float32)
    normed = (
        widened
        * lax.rsqrt(jnp.mean(widened * widened, axis=-1, keepdims=True) + EPS_RMS)
        * norm_gain
    ).astype(jnp.bfloat16)
    proj_qkv = jnp.einsum("td,ide->ite", normed, wqkv, preferred_element_type=jnp.float32)
    q_part = proj_qkv[0]
    k_part = proj_qkv[1]
    v_part = proj_qkv[2]
    square_sums = exchange_sum(
        jnp.stack([jnp.sum(q_part * q_part, axis=-1), jnp.sum(k_part * k_part, axis=-1)])
    )
    inner_width = HEADS * HD
    q_scaled = (
        q_part * lax.rsqrt(square_sums[0] / inner_width + EPS_RMS)[:, None] * qk_gain[0]
    ).astype(jnp.bfloat16)
    k_scaled = (
        k_part * lax.rsqrt(square_sums[1] / inner_width + EPS_RMS)[:, None] * qk_gain[1]
    ).astype(jnp.bfloat16)
    v_scaled = v_part.astype(jnp.bfloat16)
    heads_here = q_part.shape[1] // HD

    def split_heads(matrix):
        return matrix.reshape(seq_len, heads_here, HD).transpose(1, 0, 2)

    block_total = block_count(seq_len)
    block_rows = seq_len // block_total
    query_blocks = (
        split_heads(q_scaled).reshape(heads_here, block_total, block_rows, HD).transpose(1, 0, 2, 3)
    )
    seg_blocks = group_segs.reshape(block_total, block_rows)
    key_heads = split_heads(k_scaled)
    value_heads = split_heads(v_scaled)
    mixed = lax.map(
        lambda block_item: attend_block(
            block_item[0], key_heads, value_heads, block_item[1], group_segs
        ),
        (query_blocks, seg_blocks),
    )
    attended = mixed.transpose(0, 2, 1, 3).reshape(seq_len, heads_here * HD)
    width_dev = bproj.shape[0]
    all_heads = lax.all_gather(
        lax.all_gather(attended, "tz", axis=1, tiled=True), "ty", axis=1, tiled=True
    )
    attn_out = jnp.dot(all_heads, wproj_cols, preferred_element_type=jnp.float32)
    own_columns = lax.dynamic_slice_in_dim(gathered, tp_index * width_dev, width_dev, 1).astype(
        jnp.float32
    )
    stream = (own_columns + layer_scale * (attn_out + bproj)).astype(jnp.bfloat16)
    merged = merge_rows(stream).astype(jnp.float32)
    feature_total = 4 * D
    local_count = 4 * width_dev
    local_sum = jnp.sum(merged, axis=(1, 2))
    local_mean = local_sum / local_count
    local_dev = merged - local_mean[:, None, None]
    local_m2 = jnp.sum(local_dev * local_dev, axis=(1, 2))
    stats = exchange_gather(jnp.stack([local_sum, local_m2])[None])
    row_mean = jnp.sum(stats[:, 0], axis=0) / feature_total
    spread = stats[:, 0] / local_count - row_mean[None, :]
    row_m2 = jnp.sum(stats[:, 1], axis=0) + local_count * jnp.sum(spread * spread, axis=0)
    row_var = row_m2 / feature_total
    centered = merged - row_mean[:, None, None]
    normal_rows = (
        centered * lax.rsqrt(row_var + EPS_LN)[:, None, None] * ln_weight + ln_bias
    ).astype(jnp.bfloat16)
    merged_total = normal_rows.shape[0]
    flat_rows = normal_rows.reshape(merged_total, 4 * width_dev)
    flat_weight = w_merge.reshape(4 * width_dev, w_merge.shape[2])
    merged_dev = merged_total // tp_total
    row_part = jnp.dot(flat_rows, flat_weight, preferred_element_type=jnp.float32)
    row_outer = lax.psum_scatter(row_part.astype(jnp.bfloat16), "ty", scatter_dimension=0, tiled=True)
    own_rows = scatter_sum_exchange(row_outer, "tz", 0)
    first_tokens = merge_rows(group_segs.reshape(seq_len, 1))[:, 0, 0]
    own_first = lax.dynamic_slice_in_dim(first_tokens, tp_index * merged_dev, merged_dev, 0)
    live_rows = (own_first >= 0).astype(jnp.float32)
    out_rows = (jax.nn.gelu(own_rows + b_merge, approximate=False) * live_rows[:, None]).astype(
        jnp.bfloat16
    )
    capacity = (merged_dev + group_total - 1) // group_total + 1
    group_ids = jnp.arange(group_total, dtype=jnp.int32)
    slot_ids = jnp.arange(capacity, dtype=jnp.int32)
    mine_ids = lax.dynamic_index_in_dim(owners[:, :, 0], req_index, 0, keepdims=False)
    slot_rank = slot_ranks(mine_ids, group_total)
    selector = (mine_ids[None, None, :] == group_ids[:, None, None]) & (
        slot_rank[None, None, :] == slot_ids[None, :, None]
    )
    outgoing = jnp.einsum(
        "gcm,mf->gcf", selector.astype(jnp.bfloat16), out_rows, preferred_element_type=jnp.float32
    ).astype(jnp.bfloat16)
    incoming = lax.all_to_all(outgoing, "req", split_axis=0, concat_axis=0, tiled=True)
    return incoming.reshape(1, group_total, 1, capacity, incoming.shape[-1])


def solution(mesh):
    grid = mesh.devices
    inner = 4 if grid.shape[1] % 4 == 0 else 1
    split = Mesh(
        grid.reshape(grid.shape[0], grid.shape[1] // inner, inner), ("req",) + TP_AXES
    )
    tp = TP_AXES
    placed = (
        P("req", tp, None),
        P("req", None),
        P(),
        P(None, None, tp),
        P(None, tp),
        P(tp, None),
        P(tp),
        P(tp),
        P(None, tp),
        P(None, tp),
        P(None, tp, None),
        P(),
        P(None, tp, None),
    )
    return jax.shard_map(
        per_device,
        mesh=split,
        in_specs=placed,
        out_specs=P("req", None, tp, None, None),
        check_vma=False,
    )
```

```python
import jax
import jax.numpy as jnp
from jax import lax
from jax.sharding import Mesh
from jax.sharding import PartitionSpec as P

D = 3200
HEADS = 16
HD = 128
PW = 32


EPS_RMS = 1e-06
EPS_LN = 1e-05

TP_AXES = ("ty", "tz")


def block_count(length):
    number = max(1, length // 512)
    while length % number:
        number = number - 1
    return number


def attend_block(query_rows, key_heads, value_heads, query_segs, key_segs):
    scores = jnp.einsum(
        "hqd,hkd->hqk", query_rows, key_heads, preferred_element_type=jnp.float32
    ) * HD ** (-0.5)
    same_image = query_segs[:, None] == key_segs[None, :]
    scores = jnp.where(same_image[None], scores, -jnp.inf)
    row_max = jnp.max(scores, axis=-1, keepdims=True)
    weights = jnp.exp(scores - row_max)
    probabilities = (weights / jnp.sum(weights, axis=-1, keepdims=True)).astype(jnp.bfloat16)
    mixed = jnp.einsum(
        "hqk,hkd->hqd", probabilities, value_heads, preferred_element_type=jnp.float32
    )
    return mixed.astype(jnp.bfloat16)


def merge_rows(stream):
    feature_count = stream.shape[-1]
    shaped = stream.reshape(stream.shape[0] // (2 * PW), 2, PW // 2, 2, feature_count)
    return shaped.transpose(0, 2, 1, 3, 4).reshape(stream.shape[0] // 4, 4, feature_count)


def slot_ranks(owner_ids, group_total):
    owner_hits = (owner_ids[:, None] == jnp.arange(group_total, dtype=jnp.int32)[None, :]).astype(
        jnp.int32
    )
    before = jnp.cumsum(owner_hits, axis=0) - owner_hits
    return jnp.sum(before * owner_hits, axis=1)


def axis_exchange(value, axis_name):
    count = lax.axis_size(axis_name)
    got = [value]
    for shift in range(1, count):
        ring = [(i, (i + shift) % count) for i in range(count)]
        got.append(lax.ppermute(value, axis_name, ring))
    return got


def tp_gather(value, axis):
    count = lax.axis_size("tz")
    got = axis_exchange(value, "tz")
    ordered = jnp.stack([got[(count - k) % count] for k in range(count)], axis=0)
    ordered = jnp.roll(ordered, lax.axis_index("tz"), axis=0)
    inner = jnp.concatenate([ordered[k] for k in range(count)], axis=axis)
    return lax.all_gather(inner, "ty", axis=axis, tiled=True)


def exchange_sum(value):
    for axis_name in ("tz", "ty"):
        got = axis_exchange(value, axis_name)
        value = sum(got[1:], got[0])
    return value


def exchange_gather(value):
    for axis_name in ("tz", "ty"):
        value = jnp.concatenate(axis_exchange(value, axis_name), axis=0)
    return value


def tp_scatter_sum(value, axis):
    outer = lax.psum_scatter(value, "ty", scatter_dimension=axis, tiled=True)
    return lax.psum_scatter(outer, "tz", scatter_dimension=axis, tiled=True)


def scatter_sum_exchange(value, axis_name, axis):
    count = lax.axis_size(axis_name)
    shape = value.shape
    parts = value.reshape(shape[:axis] + (count, shape[axis] // count) + shape[axis + 1 :])
    got = lax.all_to_all(parts, axis_name, split_axis=axis, concat_axis=axis, tiled=True)
    return jnp.sum(got.astype(jnp.float32), axis=axis)


def butterfly_gather(value):
    out = value
    for axis_name in ("tz", "ty"):
        count = lax.axis_size(axis_name)
        step = 1
        while step < count:
            swap = [(i, i ^ step) for i in range(count)]
            out = jnp.concatenate([out, lax.ppermute(out, axis_name, swap)], axis=0)
            step = step * 2
    return out


def column_shards_z(weight):
    ty_count = lax.axis_size("ty")
    tz_count = lax.axis_size("tz")
    rows, cols = weight.shape
    width = cols // (ty_count * tz_count)
    parts = weight.reshape(1, 1, rows, ty_count, tz_count, width)
    return lax.all_to_all(parts, "tz", split_axis=4, concat_axis=1, tiled=True)


def column_shards_y(parts):
    parts = lax.all_to_all(parts, "ty", split_axis=3, concat_axis=0, tiled=True)
    return parts.reshape(-1, parts.shape[-1])


def req_exchange(outgoing):
    count = lax.axis_size("req")
    mine = lax.axis_index("req")
    ahead = jnp.roll(outgoing, -mine, axis=0)
    got = [ahead[0]]
    for shift in range(1, count):
        ring = [(i, (i + shift) % count) for i in range(count)]
        got.append(lax.ppermute(ahead[shift], "req", ring))
    ordered = jnp.stack([got[(count - k) % count] for k in range(count)], axis=0)
    return jnp.roll(ordered, mine, axis=0)


def per_device(
    tokens,
    segments,
    norm_gain,
    wqkv,
    qk_gain,
    wproj,
    bproj,
    layer_scale,
    ln_weight,
    ln_bias,
    w_merge,
    b_merge,
    owners,
):
    tp_total = lax.axis_size("ty") * lax.axis_size("tz")
    tp_index = lax.axis_index("ty") * lax.axis_size("tz") + lax.axis_index("tz")
    req_index = lax.axis_index("req")
    group_total = lax.axis_size("req")
    gathered, wproj_half = lax.optimization_barrier((tp_gather(tokens, 1)[0], column_shards_z(wproj)))
    seq_len = gathered.shape[0]
    group_segs = segments[0]
    widened = gathered.astype(jnp.float32)
    normed = (
        widened
        * lax.rsqrt(jnp.mean(widened * widened, axis=-1, keepdims=True) + EPS_RMS)
        * norm_gain
    ).astype(jnp.bfloat16)
    proj_qkv = jnp.einsum("td,ide->ite", normed, wqkv, preferred_element_type=jnp.float32)
    q_part = proj_qkv[0]
    k_part = proj_qkv[1]
    v_part = proj_qkv[2]
    square_sums = exchange_sum(
        jnp.stack([jnp.sum(q_part * q_part, axis=-1), jnp.sum(k_part * k_part, axis=-1)])
    )
    inner_width = HEADS * HD
    q_scaled = (
        q_part * lax.rsqrt(square_sums[0] / inner_width + EPS_RMS)[:, None] * qk_gain[0]
    ).astype(jnp.bfloat16)
    k_scaled = (
        k_part * lax.rsqrt(square_sums[1] / inner_width + EPS_RMS)[:, None] * qk_gain[1]
    ).astype(jnp.bfloat16)
    v_scaled = v_part.astype(jnp.bfloat16)
    heads_here = q_part.shape[1] // HD

    def split_heads(matrix):
        return matrix.reshape(seq_len, heads_here, HD).transpose(1, 0, 2)

    block_total = block_count(seq_len)
    block_rows = seq_len // block_total
    query_blocks = (
        split_heads(q_scaled).reshape(heads_here, block_total, block_rows, HD).transpose(1, 0, 2, 3)
    )
    seg_blocks = group_segs.reshape(block_total, block_rows)
    key_heads = split_heads(k_scaled)
    value_heads = split_heads(v_scaled)
    mixed = lax.map(
        lambda block_item: attend_block(
            block_item[0], key_heads, value_heads, block_item[1], group_segs
        ),
        (query_blocks, seg_blocks),
    )
    attended = mixed.transpose(0, 2, 1, 3).reshape(seq_len, heads_here * HD)
    width_dev = bproj.shape[0]
    all_heads = lax.all_gather(
        lax.all_gather(attended, "tz", axis=1, tiled=True), "ty", axis=1, tiled=True
    )
    wproj_cols = column_shards_y(wproj_half)
    attn_out = jnp.dot(all_heads, wproj_cols, preferred_element_type=jnp.float32)
    own_columns = lax.dynamic_slice_in_dim(gathered, tp_index * width_dev, width_dev, 1).astype(
        jnp.float32
    )
    stream = (own_columns + layer_scale * (attn_out + bproj)).astype(jnp.bfloat16)
    merged = merge_rows(stream).astype(jnp.float32)
    feature_total = 4 * D
    local_count = 4 * width_dev
    local_sum = jnp.sum(merged, axis=(1, 2))
    local_mean = local_sum / local_count
    local_dev = merged - local_mean[:, None, None]
    local_m2 = jnp.sum(local_dev * local_dev, axis=(1, 2))
    stats = exchange_gather(jnp.stack([local_sum, local_m2])[None])
    row_mean = jnp.sum(stats[:, 0], axis=0) / feature_total
    spread = stats[:, 0] / local_count - row_mean[None, :]
    row_m2 = jnp.sum(stats[:, 1], axis=0) + local_count * jnp.sum(spread * spread, axis=0)
    row_var = row_m2 / feature_total
    centered = merged - row_mean[:, None, None]
    normal_rows = (
        centered * lax.rsqrt(row_var + EPS_LN)[:, None, None] * ln_weight + ln_bias
    ).astype(jnp.bfloat16)
    merged_total = normal_rows.shape[0]
    flat_rows = normal_rows.reshape(merged_total, 4 * width_dev)
    flat_weight = w_merge.reshape(4 * width_dev, w_merge.shape[2])
    merged_dev = merged_total // tp_total
    row_part = jnp.dot(flat_rows, flat_weight, preferred_element_type=jnp.float32)
    row_outer = lax.psum_scatter(row_part.astype(jnp.bfloat16), "ty", scatter_dimension=0, tiled=True)
    own_rows = scatter_sum_exchange(row_outer, "tz", 0)
    first_tokens = merge_rows(group_segs.reshape(seq_len, 1))[:, 0, 0]
    own_first = lax.dynamic_slice_in_dim(first_tokens, tp_index * merged_dev, merged_dev, 0)
    live_rows = (own_first >= 0).astype(jnp.float32)
    out_rows = (jax.nn.gelu(own_rows + b_merge, approximate=False) * live_rows[:, None]).astype(
        jnp.bfloat16
    )
    capacity = (merged_dev + group_total - 1) // group_total + 1
    group_ids = jnp.arange(group_total, dtype=jnp.int32)
    slot_ids = jnp.arange(capacity, dtype=jnp.int32)
    mine_ids = lax.dynamic_index_in_dim(owners[:, :, 0], req_index, 0, keepdims=False)
    slot_rank = slot_ranks(mine_ids, group_total)
    selector = (mine_ids[None, None, :] == group_ids[:, None, None]) & (
        slot_rank[None, None, :] == slot_ids[None, :, None]
    )
    outgoing = jnp.einsum(
        "gcm,mf->gcf", selector.astype(jnp.bfloat16), out_rows, preferred_element_type=jnp.float32
    ).astype(jnp.bfloat16)
    incoming = lax.all_to_all(outgoing, "req", split_axis=0, concat_axis=0, tiled=True)
    return incoming.reshape(1, group_total, 1, capacity, incoming.shape[-1])


def solution(mesh):
    grid = mesh.devices
    inner = 4 if grid.shape[1] % 4 == 0 else 1
    split = Mesh(
        grid.reshape(grid.shape[0], grid.shape[1] // inner, inner), ("req",) + TP_AXES
    )
    tp = TP_AXES
    placed = (
        P("req", tp, None),
        P("req", None),
        P(),
        P(None, None, tp),
        P(None, tp),
        P(tp, None),
        P(tp),
        P(tp),
        P(None, tp),
        P(None, tp),
        P(None, tp, None),
        P(),
        P(None, tp, None),
    )
    return jax.shard_map(
        per_device,
        mesh=split,
        in_specs=placed,
        out_specs=P("req", None, tp, None, None),
        check_vma=False,
    )
```

```python
import jax
import jax.numpy as jnp
from jax import lax
from jax.sharding import Mesh
from jax.sharding import PartitionSpec as P

D = 3200
HEADS = 16
HD = 128
PW = 32


EPS_RMS = 1e-06
EPS_LN = 1e-05

TP_AXES = ("ty", "tz")


def block_count(length):
    number = max(1, length // 512)
    while length % number:
        number = number - 1
    return number


def attend_block(query_rows, key_heads, value_heads, query_segs, key_segs):
    scores = jnp.einsum(
        "hqd,hkd->hqk", query_rows, key_heads, preferred_element_type=jnp.float32
    ) * HD ** (-0.5)
    same_image = query_segs[:, None] == key_segs[None, :]
    scores = jnp.where(same_image[None], scores, -jnp.inf)
    row_max = jnp.max(scores, axis=-1, keepdims=True)
    weights = jnp.exp(scores - row_max)
    probabilities = (weights / jnp.sum(weights, axis=-1, keepdims=True)).astype(jnp.bfloat16)
    mixed = jnp.einsum(
        "hqk,hkd->hqd", probabilities, value_heads, preferred_element_type=jnp.float32
    )
    return mixed.astype(jnp.bfloat16)


def merge_rows(stream):
    feature_count = stream.shape[-1]
    shaped = stream.reshape(stream.shape[0] // (2 * PW), 2, PW // 2, 2, feature_count)
    return shaped.transpose(0, 2, 1, 3, 4).reshape(stream.shape[0] // 4, 4, feature_count)


def slot_ranks(owner_ids, group_total):
    owner_hits = (owner_ids[:, None] == jnp.arange(group_total, dtype=jnp.int32)[None, :]).astype(
        jnp.int32
    )
    before = jnp.cumsum(owner_hits, axis=0) - owner_hits
    return jnp.sum(before * owner_hits, axis=1)


def axis_exchange(value, axis_name):
    count = lax.axis_size(axis_name)
    got = [value]
    for shift in range(1, count):
        ring = [(i, (i + shift) % count) for i in range(count)]
        got.append(lax.ppermute(value, axis_name, ring))
    return got


def tp_gather(value, axis):
    count = lax.axis_size("tz")
    got = axis_exchange(value, "tz")
    ordered = jnp.stack([got[(count - k) % count] for k in range(count)], axis=0)
    ordered = jnp.roll(ordered, lax.axis_index("tz"), axis=0)
    inner = jnp.concatenate([ordered[k] for k in range(count)], axis=axis)
    return lax.all_gather(inner, "ty", axis=axis, tiled=True)


def exchange_sum(value):
    for axis_name in ("tz", "ty"):
        got = axis_exchange(value, axis_name)
        value = sum(got[1:], got[0])
    return value


def exchange_gather(value):
    for axis_name in ("tz", "ty"):
        value = jnp.concatenate(axis_exchange(value, axis_name), axis=0)
    return value


def tp_scatter_sum(value, axis):
    outer = lax.psum_scatter(value, "ty", scatter_dimension=axis, tiled=True)
    return lax.psum_scatter(outer, "tz", scatter_dimension=axis, tiled=True)


def scatter_sum_exchange(value, axis_name, axis):
    count = lax.axis_size(axis_name)
    shape = value.shape
    parts = value.reshape(shape[:axis] + (count, shape[axis] // count) + shape[axis + 1 :])
    got = lax.all_to_all(parts, axis_name, split_axis=axis, concat_axis=axis, tiled=True)
    return jnp.sum(got.astype(jnp.float32), axis=axis)


def butterfly_gather(value):
    out = value
    for axis_name in ("tz", "ty"):
        count = lax.axis_size(axis_name)
        step = 1
        while step < count:
            swap = [(i, i ^ step) for i in range(count)]
            out = jnp.concatenate([out, lax.ppermute(out, axis_name, swap)], axis=0)
            step = step * 2
    return out


def head_group_columns(weight):
    ty_count = lax.axis_size("ty")
    tz_count = lax.axis_size("tz")
    rows, cols = weight.shape
    width = cols // (ty_count * tz_count)
    parts = weight.reshape(1, rows, ty_count, tz_count, width)
    parts = lax.all_to_all(parts, "tz", split_axis=3, concat_axis=0, tiled=True)
    return parts.reshape(tz_count * rows, ty_count * width)


def req_exchange(outgoing):
    count = lax.axis_size("req")
    mine = lax.axis_index("req")
    ahead = jnp.roll(outgoing, -mine, axis=0)
    got = [ahead[0]]
    for shift in range(1, count):
        ring = [(i, (i + shift) % count) for i in range(count)]
        got.append(lax.ppermute(ahead[shift], "req", ring))
    ordered = jnp.stack([got[(count - k) % count] for k in range(count)], axis=0)
    return jnp.roll(ordered, mine, axis=0)


def per_device(
    tokens,
    segments,
    norm_gain,
    wqkv,
    qk_gain,
    wproj,
    bproj,
    layer_scale,
    ln_weight,
    ln_bias,
    w_merge,
    b_merge,
    owners,
):
    tp_total = lax.axis_size("ty") * lax.axis_size("tz")
    tp_index = lax.axis_index("ty") * lax.axis_size("tz") + lax.axis_index("tz")
    req_index = lax.axis_index("req")
    group_total = lax.axis_size("req")
    gathered, wproj_group = lax.optimization_barrier(
        (tp_gather(tokens, 1)[0], head_group_columns(wproj))
    )
    seq_len = gathered.shape[0]
    group_segs = segments[0]
    widened = gathered.astype(jnp.float32)
    normed = (
        widened
        * lax.rsqrt(jnp.mean(widened * widened, axis=-1, keepdims=True) + EPS_RMS)
        * norm_gain
    ).astype(jnp.bfloat16)
    proj_qkv = jnp.einsum("td,ide->ite", normed, wqkv, preferred_element_type=jnp.float32)
    q_part = proj_qkv[0]
    k_part = proj_qkv[1]
    v_part = proj_qkv[2]
    square_sums = exchange_sum(
        jnp.stack([jnp.sum(q_part * q_part, axis=-1), jnp.sum(k_part * k_part, axis=-1)])
    )
    inner_width = HEADS * HD
    q_scaled = (
        q_part * lax.rsqrt(square_sums[0] / inner_width + EPS_RMS)[:, None] * qk_gain[0]
    ).astype(jnp.bfloat16)
    k_scaled = (
        k_part * lax.rsqrt(square_sums[1] / inner_width + EPS_RMS)[:, None] * qk_gain[1]
    ).astype(jnp.bfloat16)
    v_scaled = v_part.astype(jnp.bfloat16)
    heads_here = q_part.shape[1] // HD

    def split_heads(matrix):
        return matrix.reshape(seq_len, heads_here, HD).transpose(1, 0, 2)

    block_total = block_count(seq_len)
    block_rows = seq_len // block_total
    query_blocks = (
        split_heads(q_scaled).reshape(heads_here, block_total, block_rows, HD).transpose(1, 0, 2, 3)
    )
    seg_blocks = group_segs.reshape(block_total, block_rows)
    key_heads = split_heads(k_scaled)
    value_heads = split_heads(v_scaled)
    mixed = lax.map(
        lambda block_item: attend_block(
            block_item[0], key_heads, value_heads, block_item[1], group_segs
        ),
        (query_blocks, seg_blocks),
    )
    attended = mixed.transpose(0, 2, 1, 3).reshape(seq_len, heads_here * HD)
    width_dev = bproj.shape[0]
    group_heads = lax.all_gather(attended, "tz", axis=1, tiled=True)
    group_part = jnp.dot(group_heads, wproj_group, preferred_element_type=jnp.float32)
    attn_out = lax.psum_scatter(
        group_part.astype(jnp.bfloat16), "ty", scatter_dimension=1, tiled=True
    ).astype(jnp.float32)
    own_columns = lax.dynamic_slice_in_dim(gathered, tp_index * width_dev, width_dev, 1).astype(
        jnp.float32
    )
    stream = (own_columns + layer_scale * (attn_out + bproj)).astype(jnp.bfloat16)
    merged = merge_rows(stream).astype(jnp.float32)
    feature_total = 4 * D
    local_count = 4 * width_dev
    local_sum = jnp.sum(merged, axis=(1, 2))
    local_mean = local_sum / local_count
    local_dev = merged - local_mean[:, None, None]
    local_m2 = jnp.sum(local_dev * local_dev, axis=(1, 2))
    stats = exchange_gather(jnp.stack([local_sum, local_m2])[None])
    row_mean = jnp.sum(stats[:, 0], axis=0) / feature_total
    spread = stats[:, 0] / local_count - row_mean[None, :]
    row_m2 = jnp.sum(stats[:, 1], axis=0) + local_count * jnp.sum(spread * spread, axis=0)
    row_var = row_m2 / feature_total
    centered = merged - row_mean[:, None, None]
    normal_rows = (
        centered * lax.rsqrt(row_var + EPS_LN)[:, None, None] * ln_weight + ln_bias
    ).astype(jnp.bfloat16)
    merged_total = normal_rows.shape[0]
    flat_rows = normal_rows.reshape(merged_total, 4 * width_dev)
    flat_weight = w_merge.reshape(4 * width_dev, w_merge.shape[2])
    merged_dev = merged_total // tp_total
    row_part = jnp.dot(flat_rows, flat_weight, preferred_element_type=jnp.float32)
    row_outer = lax.psum_scatter(row_part.astype(jnp.bfloat16), "ty", scatter_dimension=0, tiled=True)
    own_rows = scatter_sum_exchange(row_outer, "tz", 0)
    first_tokens = merge_rows(group_segs.reshape(seq_len, 1))[:, 0, 0]
    own_first = lax.dynamic_slice_in_dim(first_tokens, tp_index * merged_dev, merged_dev, 0)
    live_rows = (own_first >= 0).astype(jnp.float32)
    out_rows = (jax.nn.gelu(own_rows + b_merge, approximate=False) * live_rows[:, None]).astype(
        jnp.bfloat16
    )
    capacity = (merged_dev + group_total - 1) // group_total + 1
    group_ids = jnp.arange(group_total, dtype=jnp.int32)
    slot_ids = jnp.arange(capacity, dtype=jnp.int32)
    mine_ids = lax.dynamic_index_in_dim(owners[:, :, 0], req_index, 0, keepdims=False)
    slot_rank = slot_ranks(mine_ids, group_total)
    selector = (mine_ids[None, None, :] == group_ids[:, None, None]) & (
        slot_rank[None, None, :] == slot_ids[None, :, None]
    )
    outgoing = jnp.einsum(
        "gcm,mf->gcf", selector.astype(jnp.bfloat16), out_rows, preferred_element_type=jnp.float32
    ).astype(jnp.bfloat16)
    incoming = lax.all_to_all(outgoing, "req", split_axis=0, concat_axis=0, tiled=True)
    return incoming.reshape(1, group_total, 1, capacity, incoming.shape[-1])


def solution(mesh):
    grid = mesh.devices
    inner = 4 if grid.shape[1] % 4 == 0 else 1
    split = Mesh(
        grid.reshape(grid.shape[0], grid.shape[1] // inner, inner), ("req",) + TP_AXES
    )
    tp = TP_AXES
    placed = (
        P("req", tp, None),
        P("req", None),
        P(),
        P(None, None, tp),
        P(None, tp),
        P(tp, None),
        P(tp),
        P(tp),
        P(None, tp),
        P(None, tp),
        P(None, tp, None),
        P(),
        P(None, tp, None),
    )
    return jax.shard_map(
        per_device,
        mesh=split,
        in_specs=placed,
        out_specs=P("req", None, tp, None, None),
        check_vma=False,
    )
```

```python
import jax
import jax.numpy as jnp
from jax import lax
from jax.sharding import Mesh
from jax.sharding import PartitionSpec as P

D = 3200
HEADS = 16
HD = 128
PW = 32


EPS_RMS = 1e-06
EPS_LN = 1e-05

TP_AXES = ("ty", "tz")


def block_count(length):
    number = max(1, length // 512)
    while length % number:
        number = number - 1
    return number


def attend_block(query_rows, key_heads, value_heads, query_segs, key_segs):
    scores = jnp.einsum(
        "hqd,hkd->hqk", query_rows, key_heads, preferred_element_type=jnp.float32
    ) * HD ** (-0.5)
    same_image = query_segs[:, None] == key_segs[None, :]
    scores = jnp.where(same_image[None], scores, -jnp.inf)
    row_max = jnp.max(scores, axis=-1, keepdims=True)
    weights = jnp.exp(scores - row_max)
    probabilities = (weights / jnp.sum(weights, axis=-1, keepdims=True)).astype(jnp.bfloat16)
    mixed = jnp.einsum(
        "hqk,hkd->hqd", probabilities, value_heads, preferred_element_type=jnp.float32
    )
    return mixed.astype(jnp.bfloat16)


def merge_rows(stream):
    feature_count = stream.shape[-1]
    shaped = stream.reshape(stream.shape[0] // (2 * PW), 2, PW // 2, 2, feature_count)
    return shaped.transpose(0, 2, 1, 3, 4).reshape(stream.shape[0] // 4, 4, feature_count)


def slot_ranks(owner_ids, group_total):
    owner_hits = (owner_ids[:, None] == jnp.arange(group_total, dtype=jnp.int32)[None, :]).astype(
        jnp.int32
    )
    before = jnp.cumsum(owner_hits, axis=0) - owner_hits
    return jnp.sum(before * owner_hits, axis=1)


def axis_exchange(value, axis_name):
    count = lax.axis_size(axis_name)
    got = [value]
    for shift in range(1, count):
        ring = [(i, (i + shift) % count) for i in range(count)]
        got.append(lax.ppermute(value, axis_name, ring))
    return got


def tp_gather(value, axis):
    count = lax.axis_size("tz")
    got = axis_exchange(value, "tz")
    ordered = jnp.stack([got[(count - k) % count] for k in range(count)], axis=0)
    ordered = jnp.roll(ordered, lax.axis_index("tz"), axis=0)
    inner = jnp.concatenate([ordered[k] for k in range(count)], axis=axis)
    return lax.all_gather(inner, "ty", axis=axis, tiled=True)


def axis_copies(value, axis_name):
    count = lax.axis_size(axis_name)
    copies = jnp.broadcast_to(value[None], (count,) + value.shape)
    return lax.all_to_all(copies, axis_name, split_axis=0, concat_axis=0, tiled=True)


def exchange_sum(value):
    for axis_name in ("tz", "ty"):
        value = jnp.sum(axis_copies(value, axis_name), axis=0)
    return value


def exchange_gather(value):
    for axis_name in ("tz", "ty"):
        got = axis_copies(value, axis_name)
        value = got.reshape((-1,) + got.shape[2:])
    return value


def scatter_sum_exchange(value, axis_name, axis):
    count = lax.axis_size(axis_name)
    shape = value.shape
    parts = value.reshape(shape[:axis] + (count, shape[axis] // count) + shape[axis + 1 :])
    got = lax.all_to_all(parts, axis_name, split_axis=axis, concat_axis=axis, tiled=True)
    return jnp.sum(got.astype(jnp.float32), axis=axis)


def head_group_columns(weight):
    ty_count = lax.axis_size("ty")
    tz_count = lax.axis_size("tz")
    rows, cols = weight.shape
    width = cols // (ty_count * tz_count)
    parts = weight.reshape(1, rows, ty_count, tz_count, width)
    parts = lax.all_to_all(parts, "tz", split_axis=3, concat_axis=0, tiled=True)
    return parts.reshape(tz_count * rows, ty_count * width)


def req_exchange(outgoing):
    count = lax.axis_size("req")
    mine = lax.axis_index("req")
    ahead = jnp.roll(outgoing, -mine, axis=0)
    got = [ahead[0]]
    for shift in range(1, count):
        ring = [(i, (i + shift) % count) for i in range(count)]
        got.append(lax.ppermute(ahead[shift], "req", ring))
    ordered = jnp.stack([got[(count - k) % count] for k in range(count)], axis=0)
    return jnp.roll(ordered, mine, axis=0)


def per_device(
    tokens,
    segments,
    norm_gain,
    wqkv,
    qk_gain,
    wproj,
    bproj,
    layer_scale,
    ln_weight,
    ln_bias,
    w_merge,
    b_merge,
    owners,
):
    tp_total = lax.axis_size("ty") * lax.axis_size("tz")
    tp_index = lax.axis_index("ty") * lax.axis_size("tz") + lax.axis_index("tz")
    req_index = lax.axis_index("req")
    group_total = lax.axis_size("req")
    gathered, wproj_group = lax.optimization_barrier(
        (tp_gather(tokens, 1)[0], head_group_columns(wproj))
    )
    seq_len = gathered.shape[0]
    group_segs = segments[0]
    widened = gathered.astype(jnp.float32)
    normed = (
        widened
        * lax.rsqrt(jnp.mean(widened * widened, axis=-1, keepdims=True) + EPS_RMS)
        * norm_gain
    ).astype(jnp.bfloat16)
    proj_qkv = jnp.einsum("td,ide->ite", normed, wqkv, preferred_element_type=jnp.float32)
    q_part = proj_qkv[0]
    k_part = proj_qkv[1]
    v_part = proj_qkv[2]
    square_sums = exchange_sum(
        jnp.stack([jnp.sum(q_part * q_part, axis=-1), jnp.sum(k_part * k_part, axis=-1)])
    )
    inner_width = HEADS * HD
    q_scaled = (
        q_part * lax.rsqrt(square_sums[0] / inner_width + EPS_RMS)[:, None] * qk_gain[0]
    ).astype(jnp.bfloat16)
    k_scaled = (
        k_part * lax.rsqrt(square_sums[1] / inner_width + EPS_RMS)[:, None] * qk_gain[1]
    ).astype(jnp.bfloat16)
    v_scaled = v_part.astype(jnp.bfloat16)
    heads_here = q_part.shape[1] // HD

    def split_heads(matrix):
        return matrix.reshape(seq_len, heads_here, HD).transpose(1, 0, 2)

    block_total = block_count(seq_len)
    block_rows = seq_len // block_total
    query_blocks = (
        split_heads(q_scaled).reshape(heads_here, block_total, block_rows, HD).transpose(1, 0, 2, 3)
    )
    seg_blocks = group_segs.reshape(block_total, block_rows)
    key_heads = split_heads(k_scaled)
    value_heads = split_heads(v_scaled)
    mixed = lax.map(
        lambda block_item: attend_block(
            block_item[0], key_heads, value_heads, block_item[1], group_segs
        ),
        (query_blocks, seg_blocks),
    )
    attended = mixed.transpose(0, 2, 1, 3).reshape(seq_len, heads_here * HD)
    width_dev = bproj.shape[0]
    group_heads = lax.all_gather(attended, "tz", axis=1, tiled=True)
    group_part = jnp.dot(group_heads, wproj_group, preferred_element_type=jnp.float32)
    attn_out = lax.psum_scatter(
        group_part.astype(jnp.bfloat16), "ty", scatter_dimension=1, tiled=True
    ).astype(jnp.float32)
    own_columns = lax.dynamic_slice_in_dim(gathered, tp_index * width_dev, width_dev, 1).astype(
        jnp.float32
    )
    stream = (own_columns + layer_scale * (attn_out + bproj)).astype(jnp.bfloat16)
    merged = merge_rows(stream).astype(jnp.float32)
    feature_total = 4 * D
    local_count = 4 * width_dev
    local_sum = jnp.sum(merged, axis=(1, 2))
    local_mean = local_sum / local_count
    local_dev = merged - local_mean[:, None, None]
    local_m2 = jnp.sum(local_dev * local_dev, axis=(1, 2))
    stats = exchange_gather(jnp.stack([local_sum, local_m2])[None])
    row_mean = jnp.sum(stats[:, 0], axis=0) / feature_total
    spread = stats[:, 0] / local_count - row_mean[None, :]
    row_m2 = jnp.sum(stats[:, 1], axis=0) + local_count * jnp.sum(spread * spread, axis=0)
    row_var = row_m2 / feature_total
    centered = merged - row_mean[:, None, None]
    normal_rows = (
        centered * lax.rsqrt(row_var + EPS_LN)[:, None, None] * ln_weight + ln_bias
    ).astype(jnp.bfloat16)
    merged_total = normal_rows.shape[0]
    flat_rows = normal_rows.reshape(merged_total, 4 * width_dev)
    flat_weight = w_merge.reshape(4 * width_dev, w_merge.shape[2])
    merged_dev = merged_total // tp_total
    row_part = jnp.dot(flat_rows, flat_weight, preferred_element_type=jnp.float32)
    row_outer = lax.psum_scatter(row_part.astype(jnp.bfloat16), "ty", scatter_dimension=0, tiled=True)
    own_rows = scatter_sum_exchange(row_outer, "tz", 0)
    first_tokens = merge_rows(group_segs.reshape(seq_len, 1))[:, 0, 0]
    own_first = lax.dynamic_slice_in_dim(first_tokens, tp_index * merged_dev, merged_dev, 0)
    live_rows = (own_first >= 0).astype(jnp.float32)
    out_rows = (jax.nn.gelu(own_rows + b_merge, approximate=False) * live_rows[:, None]).astype(
        jnp.bfloat16
    )
    capacity = (merged_dev + group_total - 1) // group_total + 1
    group_ids = jnp.arange(group_total, dtype=jnp.int32)
    slot_ids = jnp.arange(capacity, dtype=jnp.int32)
    mine_ids = lax.dynamic_index_in_dim(owners[:, :, 0], req_index, 0, keepdims=False)
    slot_rank = slot_ranks(mine_ids, group_total)
    selector = (mine_ids[None, None, :] == group_ids[:, None, None]) & (
        slot_rank[None, None, :] == slot_ids[None, :, None]
    )
    outgoing = jnp.einsum(
        "gcm,mf->gcf", selector.astype(jnp.bfloat16), out_rows, preferred_element_type=jnp.float32
    ).astype(jnp.bfloat16)
    incoming = req_exchange(outgoing)
    return incoming.reshape(1, group_total, 1, capacity, incoming.shape[-1])


def solution(mesh):
    grid = mesh.devices
    inner = 4 if grid.shape[1] % 4 == 0 else 1
    split = Mesh(
        grid.reshape(grid.shape[0], grid.shape[1] // inner, inner), ("req",) + TP_AXES
    )
    tp = TP_AXES
    placed = (
        P("req", tp, None),
        P("req", None),
        P(),
        P(None, None, tp),
        P(None, tp),
        P(tp, None),
        P(tp),
        P(tp),
        P(None, tp),
        P(None, tp),
        P(None, tp, None),
        P(),
        P(None, tp, None),
    )
    return jax.shard_map(
        per_device,
        mesh=split,
        in_specs=placed,
        out_specs=P("req", None, tp, None, None),
        check_vma=False,
    )
```

```python
import jax
import jax.numpy as jnp
from jax import lax
from jax.sharding import Mesh
from jax.sharding import PartitionSpec as P

D = 3200
HEADS = 16
HD = 128
PW = 32


EPS_RMS = 1e-06
EPS_LN = 1e-05

TP_AXES = ("ty", "tz")


def block_count(length):
    number = max(1, length // 512)
    while length % number:
        number = number - 1
    return number


def attend_block(query_rows, key_heads, value_heads, query_segs, key_segs):
    scores = jnp.einsum(
        "hqd,hkd->hqk", query_rows, key_heads, preferred_element_type=jnp.float32
    ) * HD ** (-0.5)
    same_image = query_segs[:, None] == key_segs[None, :]
    scores = jnp.where(same_image[None], scores, -jnp.inf)
    row_max = jnp.max(scores, axis=-1, keepdims=True)
    weights = jnp.exp(scores - row_max)
    probabilities = (weights / jnp.sum(weights, axis=-1, keepdims=True)).astype(jnp.bfloat16)
    mixed = jnp.einsum(
        "hqk,hkd->hqd", probabilities, value_heads, preferred_element_type=jnp.float32
    )
    return mixed.astype(jnp.bfloat16)


def merge_rows(stream):
    feature_count = stream.shape[-1]
    shaped = stream.reshape(stream.shape[0] // (2 * PW), 2, PW // 2, 2, feature_count)
    return shaped.transpose(0, 2, 1, 3, 4).reshape(stream.shape[0] // 4, 4, feature_count)


def slot_ranks(owner_ids, group_total):
    owner_hits = (owner_ids[:, None] == jnp.arange(group_total, dtype=jnp.int32)[None, :]).astype(
        jnp.int32
    )
    before = jnp.cumsum(owner_hits, axis=0) - owner_hits
    return jnp.sum(before * owner_hits, axis=1)


def axis_exchange(value, axis_name):
    count = lax.axis_size(axis_name)
    got = [value]
    for shift in range(1, count):
        ring = [(i, (i + shift) % count) for i in range(count)]
        got.append(lax.ppermute(value, axis_name, ring))
    return got


def tp_gather(value, axis):
    count = lax.axis_size("tz")
    got = axis_exchange(value, "tz")
    mine = lax.axis_index("tz")
    blocks = []
    for k in range(count):
        which = (mine - k) % count
        block = got[0]
        for shift in range(1, count):
            block = jnp.where(which == shift, got[shift], block)
        blocks.append(block)
    inner = jnp.concatenate(blocks, axis=axis)
    return lax.all_gather(inner, "ty", axis=axis, tiled=True)


def exchange_sum(value):
    for axis_name in ("tz", "ty"):
        got = axis_exchange(value, axis_name)
        value = sum(got[1:], got[0])
    return value


def exchange_gather(value):
    for axis_name in ("tz", "ty"):
        value = jnp.concatenate(axis_exchange(value, axis_name), axis=0)
    return value


def tp_scatter_sum(value, axis):
    outer = lax.psum_scatter(value, "ty", scatter_dimension=axis, tiled=True)
    return lax.psum_scatter(outer, "tz", scatter_dimension=axis, tiled=True)


def scatter_sum_exchange(value, axis_name, axis):
    count = lax.axis_size(axis_name)
    shape = value.shape
    parts = value.reshape(shape[:axis] + (count, shape[axis] // count) + shape[axis + 1 :])
    got = lax.all_to_all(parts, axis_name, split_axis=axis, concat_axis=axis, tiled=True)
    return jnp.sum(got.astype(jnp.float32), axis=axis)


def butterfly_gather(value):
    out = value
    for axis_name in ("tz", "ty"):
        count = lax.axis_size(axis_name)
        step = 1
        while step < count:
            swap = [(i, i ^ step) for i in range(count)]
            out = jnp.concatenate([out, lax.ppermute(out, axis_name, swap)], axis=0)
            step = step * 2
    return out


def head_group_columns(weight):
    ty_count = lax.axis_size("ty")
    tz_count = lax.axis_size("tz")
    rows, cols = weight.shape
    width = cols // (ty_count * tz_count)
    parts = weight.reshape(1, rows, ty_count, tz_count, width)
    parts = lax.all_to_all(parts, "tz", split_axis=3, concat_axis=0, tiled=True)
    return parts.reshape(tz_count * rows, ty_count * width)


def req_exchange(outgoing):
    count = lax.axis_size("req")
    mine = lax.axis_index("req")
    ahead = jnp.roll(outgoing, -mine, axis=0)
    got = [ahead[0]]
    for shift in range(1, count):
        ring = [(i, (i + shift) % count) for i in range(count)]
        got.append(lax.ppermute(ahead[shift], "req", ring))
    ordered = jnp.stack([got[(count - k) % count] for k in range(count)], axis=0)
    return jnp.roll(ordered, mine, axis=0)


def per_device(
    tokens,
    segments,
    norm_gain,
    wqkv,
    qk_gain,
    wproj,
    bproj,
    layer_scale,
    ln_weight,
    ln_bias,
    w_merge,
    b_merge,
    owners,
):
    tp_total = lax.axis_size("ty") * lax.axis_size("tz")
    tp_index = lax.axis_index("ty") * lax.axis_size("tz") + lax.axis_index("tz")
    req_index = lax.axis_index("req")
    group_total = lax.axis_size("req")
    gathered, wproj_group = lax.optimization_barrier(
        (tp_gather(tokens, 1)[0], head_group_columns(wproj))
    )
    seq_len = gathered.shape[0]
    group_segs = segments[0]
    widened = gathered.astype(jnp.float32)
    normed = (
        widened
        * lax.rsqrt(jnp.mean(widened * widened, axis=-1, keepdims=True) + EPS_RMS)
        * norm_gain
    ).astype(jnp.bfloat16)
    proj_qkv = jnp.einsum("td,ide->ite", normed, wqkv, preferred_element_type=jnp.float32)
    q_part = proj_qkv[0]
    k_part = proj_qkv[1]
    v_part = proj_qkv[2]
    square_sums = exchange_sum(
        jnp.stack([jnp.sum(q_part * q_part, axis=-1), jnp.sum(k_part * k_part, axis=-1)])
    )
    inner_width = HEADS * HD
    q_scaled = (
        q_part * lax.rsqrt(square_sums[0] / inner_width + EPS_RMS)[:, None] * qk_gain[0]
    ).astype(jnp.bfloat16)
    k_scaled = (
        k_part * lax.rsqrt(square_sums[1] / inner_width + EPS_RMS)[:, None] * qk_gain[1]
    ).astype(jnp.bfloat16)
    v_scaled = v_part.astype(jnp.bfloat16)
    heads_here = q_part.shape[1] // HD

    def split_heads(matrix):
        return matrix.reshape(seq_len, heads_here, HD).transpose(1, 0, 2)

    block_total = block_count(seq_len)
    block_rows = seq_len // block_total
    query_blocks = (
        split_heads(q_scaled).reshape(heads_here, block_total, block_rows, HD).transpose(1, 0, 2, 3)
    )
    seg_blocks = group_segs.reshape(block_total, block_rows)
    key_heads = split_heads(k_scaled)
    value_heads = split_heads(v_scaled)
    mixed = lax.map(
        lambda block_item: attend_block(
            block_item[0], key_heads, value_heads, block_item[1], group_segs
        ),
        (query_blocks, seg_blocks),
    )
    attended = mixed.transpose(0, 2, 1, 3).reshape(seq_len, heads_here * HD)
    width_dev = bproj.shape[0]
    group_heads = lax.all_gather(attended, "tz", axis=1, tiled=True)
    group_part = jnp.dot(group_heads, wproj_group, preferred_element_type=jnp.float32)
    attn_out = lax.psum_scatter(
        group_part.astype(jnp.bfloat16), "ty", scatter_dimension=1, tiled=True
    ).astype(jnp.float32)
    own_columns = lax.dynamic_slice_in_dim(gathered, tp_index * width_dev, width_dev, 1).astype(
        jnp.float32
    )
    stream = (own_columns + layer_scale * (attn_out + bproj)).astype(jnp.bfloat16)
    merged = merge_rows(stream).astype(jnp.float32)
    feature_total = 4 * D
    local_count = 4 * width_dev
    local_sum = jnp.sum(merged, axis=(1, 2))
    local_mean = local_sum / local_count
    local_dev = merged - local_mean[:, None, None]
    local_m2 = jnp.sum(local_dev * local_dev, axis=(1, 2))
    merged_total = merged.shape[0]
    flat_weight = w_merge.reshape(4 * width_dev, w_merge.shape[2])
    local_rows = (local_dev * ln_weight).astype(jnp.bfloat16).reshape(merged_total, 4 * width_dev)
    local_part = lax.optimization_barrier(
        jnp.dot(local_rows, flat_weight, preferred_element_type=jnp.float32)
    )
    exact = lax.Precision.HIGHEST
    gain_part = jnp.dot(ln_weight.reshape(1, -1), flat_weight, precision=exact)[0]
    bias_part = jnp.dot(ln_bias.reshape(1, -1), flat_weight, precision=exact)[0]
    stats = exchange_gather(jnp.stack([local_sum, local_m2])[None])
    row_mean = jnp.sum(stats[:, 0], axis=0) / feature_total
    spread = stats[:, 0] / local_count - row_mean[None, :]
    row_m2 = jnp.sum(stats[:, 1], axis=0) + local_count * jnp.sum(spread * spread, axis=0)
    row_var = row_m2 / feature_total
    row_scale = lax.rsqrt(row_var + EPS_LN)
    shift = local_mean - row_mean
    row_part = (
        row_scale[:, None] * (local_part + shift[:, None] * gain_part[None, :]) + bias_part[None, :]
    )
    merged_dev = merged_total // tp_total
    row_outer = lax.psum_scatter(row_part.astype(jnp.bfloat16), "ty", scatter_dimension=0, tiled=True)
    own_rows = scatter_sum_exchange(row_outer, "tz", 0)
    first_tokens = merge_rows(group_segs.reshape(seq_len, 1))[:, 0, 0]
    own_first = lax.dynamic_slice_in_dim(first_tokens, tp_index * merged_dev, merged_dev, 0)
    live_rows = (own_first >= 0).astype(jnp.float32)
    out_rows = (jax.nn.gelu(own_rows + b_merge, approximate=False) * live_rows[:, None]).astype(
        jnp.bfloat16
    )
    capacity = (merged_dev + group_total - 1) // group_total + 1
    group_ids = jnp.arange(group_total, dtype=jnp.int32)
    slot_ids = jnp.arange(capacity, dtype=jnp.int32)
    mine_ids = lax.dynamic_index_in_dim(owners[:, :, 0], req_index, 0, keepdims=False)
    slot_rank = slot_ranks(mine_ids, group_total)
    selector = (mine_ids[None, None, :] == group_ids[:, None, None]) & (
        slot_rank[None, None, :] == slot_ids[None, :, None]
    )
    outgoing = jnp.einsum(
        "gcm,mf->gcf", selector.astype(jnp.bfloat16), out_rows, preferred_element_type=jnp.float32
    ).astype(jnp.bfloat16)
    incoming = lax.all_to_all(outgoing, "req", split_axis=0, concat_axis=0, tiled=True)
    return incoming.reshape(1, group_total, 1, capacity, incoming.shape[-1])


def solution(mesh):
    grid = mesh.devices
    inner = 4 if grid.shape[1] % 4 == 0 else 1
    split = Mesh(
        grid.reshape(grid.shape[0], grid.shape[1] // inner, inner), ("req",) + TP_AXES
    )
    tp = TP_AXES
    placed = (
        P("req", tp, None),
        P("req", None),
        P(),
        P(None, None, tp),
        P(None, tp),
        P(tp, None),
        P(tp),
        P(tp),
        P(None, tp),
        P(None, tp),
        P(None, tp, None),
        P(),
        P(None, tp, None),
    )
    return jax.shard_map(
        per_device,
        mesh=split,
        in_specs=placed,
        out_specs=P("req", None, tp, None, None),
        check_vma=False,
    )
```

```python
import jax
import jax.numpy as jnp
from jax import lax
from jax.sharding import Mesh
from jax.sharding import PartitionSpec as P

D = 3200
HEADS = 16
HD = 128
PW = 32


EPS_RMS = 1e-06
EPS_LN = 1e-05

TP_AXES = ("ty", "tz")


def block_count(length):
    number = max(1, length // 512)
    while length % number:
        number = number - 1
    return number


def attend_block(query_rows, key_heads, value_heads, query_segs, key_segs):
    scores = jnp.einsum(
        "hqd,hkd->hqk", query_rows, key_heads, preferred_element_type=jnp.float32
    ) * HD ** (-0.5)
    same_image = query_segs[:, None] == key_segs[None, :]
    scores = jnp.where(same_image[None], scores, -jnp.inf)
    row_max = jnp.max(scores, axis=-1, keepdims=True)
    weights = jnp.exp(scores - row_max)
    probabilities = (weights / jnp.sum(weights, axis=-1, keepdims=True)).astype(jnp.bfloat16)
    mixed = jnp.einsum(
        "hqk,hkd->hqd", probabilities, value_heads, preferred_element_type=jnp.float32
    )
    return mixed.astype(jnp.bfloat16)


def merge_rows(stream):
    feature_count = stream.shape[-1]
    shaped = stream.reshape(stream.shape[0] // (2 * PW), 2, PW // 2, 2, feature_count)
    return shaped.transpose(0, 2, 1, 3, 4).reshape(stream.shape[0] // 4, 4, feature_count)


def slot_ranks(owner_ids, group_total):
    owner_hits = (owner_ids[:, None] == jnp.arange(group_total, dtype=jnp.int32)[None, :]).astype(
        jnp.int32
    )
    before = jnp.cumsum(owner_hits, axis=0) - owner_hits
    return jnp.sum(before * owner_hits, axis=1)


def axis_exchange(value, axis_name):
    count = lax.axis_size(axis_name)
    got = [value]
    for shift in range(1, count):
        ring = [(i, (i + shift) % count) for i in range(count)]
        got.append(lax.ppermute(value, axis_name, ring))
    return got


def tp_gather(value, axis):
    count = lax.axis_size("tz")
    got = axis_exchange(value, "tz")
    mine = lax.axis_index("tz")
    blocks = []
    for k in range(count):
        which = (mine - k) % count
        block = got[0]
        for shift in range(1, count):
            block = jnp.where(which == shift, got[shift], block)
        blocks.append(block)
    inner = jnp.concatenate(blocks, axis=axis)
    return lax.all_gather(inner, "ty", axis=axis, tiled=True)


def exchange_sum(value):
    for axis_name in ("tz", "ty"):
        got = axis_exchange(value, axis_name)
        value = sum(got[1:], got[0])
    return value


def exchange_gather(value):
    for axis_name in ("tz", "ty"):
        value = jnp.concatenate(axis_exchange(value, axis_name), axis=0)
    return value


def tp_scatter_sum(value, axis):
    outer = lax.psum_scatter(value, "ty", scatter_dimension=axis, tiled=True)
    return lax.psum_scatter(outer, "tz", scatter_dimension=axis, tiled=True)


def scatter_sum_exchange(value, axis_name, axis):
    count = lax.axis_size(axis_name)
    shape = value.shape
    parts = value.reshape(shape[:axis] + (count, shape[axis] // count) + shape[axis + 1 :])
    got = lax.all_to_all(parts, axis_name, split_axis=axis, concat_axis=axis, tiled=True)
    return jnp.sum(got.astype(jnp.float32), axis=axis)


def butterfly_gather(value):
    out = value
    for axis_name in ("tz", "ty"):
        count = lax.axis_size(axis_name)
        step = 1
        while step < count:
            swap = [(i, i ^ step) for i in range(count)]
            out = jnp.concatenate([out, lax.ppermute(out, axis_name, swap)], axis=0)
            step = step * 2
    return out


def head_group_columns(weight):
    ty_count = lax.axis_size("ty")
    tz_count = lax.axis_size("tz")
    rows, cols = weight.shape
    width = cols // (ty_count * tz_count)
    parts = weight.reshape(1, rows, ty_count, tz_count, width)
    parts = lax.all_to_all(parts, "tz", split_axis=3, concat_axis=0, tiled=True)
    return parts.reshape(tz_count * rows, ty_count * width)


def req_exchange(outgoing):
    count = lax.axis_size("req")
    mine = lax.axis_index("req")
    ahead = jnp.roll(outgoing, -mine, axis=0)
    got = [ahead[0]]
    for shift in range(1, count):
        ring = [(i, (i + shift) % count) for i in range(count)]
        got.append(lax.ppermute(ahead[shift], "req", ring))
    ordered = jnp.stack([got[(count - k) % count] for k in range(count)], axis=0)
    return jnp.roll(ordered, mine, axis=0)


def per_device(
    tokens,
    segments,
    norm_gain,
    wqkv,
    qk_gain,
    wproj,
    bproj,
    layer_scale,
    ln_weight,
    ln_bias,
    w_merge,
    b_merge,
    owners,
):
    tp_total = lax.axis_size("ty") * lax.axis_size("tz")
    tp_index = lax.axis_index("ty") * lax.axis_size("tz") + lax.axis_index("tz")
    req_index = lax.axis_index("req")
    group_total = lax.axis_size("req")
    gathered, wproj_group = lax.optimization_barrier(
        (tp_gather(tokens, 1)[0], head_group_columns(wproj))
    )
    seq_len = gathered.shape[0]
    group_segs = segments[0]
    widened = gathered.astype(jnp.float32)
    normed = (
        widened
        * lax.rsqrt(jnp.mean(widened * widened, axis=-1, keepdims=True) + EPS_RMS)
        * norm_gain
    ).astype(jnp.bfloat16)
    proj_qkv = jnp.einsum("td,ide->ite", normed, wqkv, preferred_element_type=jnp.float32)
    q_part = proj_qkv[0]
    k_part = proj_qkv[1]
    v_part = proj_qkv[2]
    square_sums = exchange_sum(
        jnp.stack([jnp.sum(q_part * q_part, axis=-1), jnp.sum(k_part * k_part, axis=-1)])
    )
    inner_width = HEADS * HD
    q_scaled = (
        q_part * lax.rsqrt(square_sums[0] / inner_width + EPS_RMS)[:, None] * qk_gain[0]
    ).astype(jnp.bfloat16)
    k_scaled = (
        k_part * lax.rsqrt(square_sums[1] / inner_width + EPS_RMS)[:, None] * qk_gain[1]
    ).astype(jnp.bfloat16)
    v_scaled = v_part.astype(jnp.bfloat16)
    heads_here = q_part.shape[1] // HD

    def split_heads(matrix):
        return matrix.reshape(seq_len, heads_here, HD).transpose(1, 0, 2)

    block_total = block_count(seq_len)
    block_rows = seq_len // block_total
    query_blocks = (
        split_heads(q_scaled).reshape(heads_here, block_total, block_rows, HD).transpose(1, 0, 2, 3)
    )
    seg_blocks = group_segs.reshape(block_total, block_rows)
    key_heads = split_heads(k_scaled)
    value_heads = split_heads(v_scaled)
    mixed = lax.map(
        lambda block_item: attend_block(
            block_item[0], key_heads, value_heads, block_item[1], group_segs
        ),
        (query_blocks, seg_blocks),
    )
    attended = mixed.transpose(0, 2, 1, 3).reshape(seq_len, heads_here * HD)
    width_dev = bproj.shape[0]
    group_heads = lax.all_gather(attended, "tz", axis=1, tiled=True)
    group_part = jnp.dot(group_heads, wproj_group, preferred_element_type=jnp.float32)
    attn_out = scatter_sum_exchange(group_part.astype(jnp.bfloat16), "ty", 1)
    own_columns = lax.dynamic_slice_in_dim(gathered, tp_index * width_dev, width_dev, 1).astype(
        jnp.float32
    )
    stream = (own_columns + layer_scale * (attn_out + bproj)).astype(jnp.bfloat16)
    merged = merge_rows(stream).astype(jnp.float32)
    feature_total = 4 * D
    local_count = 4 * width_dev
    local_sum = jnp.sum(merged, axis=(1, 2))
    local_mean = local_sum / local_count
    local_dev = merged - local_mean[:, None, None]
    local_m2 = jnp.sum(local_dev * local_dev, axis=(1, 2))
    merged_total = merged.shape[0]
    flat_weight = w_merge.reshape(4 * width_dev, w_merge.shape[2])
    local_rows = (local_dev * ln_weight).astype(jnp.bfloat16).reshape(merged_total, 4 * width_dev)
    local_part = lax.optimization_barrier(
        jnp.dot(local_rows, flat_weight, preferred_element_type=jnp.float32)
    )
    exact = lax.Precision.HIGHEST
    gain_part = jnp.dot(ln_weight.reshape(1, -1), flat_weight, precision=exact)[0]
    bias_part = jnp.dot(ln_bias.reshape(1, -1), flat_weight, precision=exact)[0]
    stats = exchange_gather(jnp.stack([local_sum, local_m2])[None])
    row_mean = jnp.sum(stats[:, 0], axis=0) / feature_total
    spread = stats[:, 0] / local_count - row_mean[None, :]
    row_m2 = jnp.sum(stats[:, 1], axis=0) + local_count * jnp.sum(spread * spread, axis=0)
    row_var = row_m2 / feature_total
    row_scale = lax.rsqrt(row_var + EPS_LN)
    shift = local_mean - row_mean
    row_part = (
        row_scale[:, None] * (local_part + shift[:, None] * gain_part[None, :]) + bias_part[None, :]
    )
    merged_dev = merged_total // tp_total
    row_outer = scatter_sum_exchange(row_part.astype(jnp.bfloat16), "ty", 0)
    own_rows = scatter_sum_exchange(row_outer.astype(jnp.bfloat16), "tz", 0)
    first_tokens = merge_rows(group_segs.reshape(seq_len, 1))[:, 0, 0]
    own_first = lax.dynamic_slice_in_dim(first_tokens, tp_index * merged_dev, merged_dev, 0)
    live_rows = (own_first >= 0).astype(jnp.float32)
    out_rows = (jax.nn.gelu(own_rows + b_merge, approximate=False) * live_rows[:, None]).astype(
        jnp.bfloat16
    )
    capacity = (merged_dev + group_total - 1) // group_total + 1
    group_ids = jnp.arange(group_total, dtype=jnp.int32)
    slot_ids = jnp.arange(capacity, dtype=jnp.int32)
    mine_ids = lax.dynamic_index_in_dim(owners[:, :, 0], req_index, 0, keepdims=False)
    slot_rank = slot_ranks(mine_ids, group_total)
    selector = (mine_ids[None, None, :] == group_ids[:, None, None]) & (
        slot_rank[None, None, :] == slot_ids[None, :, None]
    )
    outgoing = jnp.einsum(
        "gcm,mf->gcf", selector.astype(jnp.bfloat16), out_rows, preferred_element_type=jnp.float32
    ).astype(jnp.bfloat16)
    incoming = lax.all_to_all(outgoing, "req", split_axis=0, concat_axis=0, tiled=True)
    return incoming.reshape(1, group_total, 1, capacity, incoming.shape[-1])


def solution(mesh):
    grid = mesh.devices
    inner = 4 if grid.shape[1] % 4 == 0 else 1
    split = Mesh(
        grid.reshape(grid.shape[0], grid.shape[1] // inner, inner), ("req",) + TP_AXES
    )
    tp = TP_AXES
    placed = (
        P("req", tp, None),
        P("req", None),
        P(),
        P(None, None, tp),
        P(None, tp),
        P(tp, None),
        P(tp),
        P(tp),
        P(None, tp),
        P(None, tp),
        P(None, tp, None),
        P(),
        P(None, tp, None),
    )
    return jax.shard_map(
        per_device,
        mesh=split,
        in_specs=placed,
        out_specs=P("req", None, tp, None, None),
        check_vma=False,
    )
```

```python
import jax
import jax.numpy as jnp
from jax import lax
from jax.sharding import Mesh
from jax.sharding import PartitionSpec as P

D = 3200
HEADS = 16
HD = 128
PW = 32


EPS_RMS = 1e-06
EPS_LN = 1e-05

TP_AXES = ("ty", "tz")


def block_count(length):
    number = max(1, length // 512)
    while length % number:
        number = number - 1
    return number


def attend_block(query_rows, key_heads, value_heads, query_segs, key_segs):
    scores = jnp.einsum(
        "hqd,hkd->hqk", query_rows, key_heads, preferred_element_type=jnp.float32
    ) * HD ** (-0.5)
    same_image = query_segs[:, None] == key_segs[None, :]
    scores = jnp.where(same_image[None], scores, -jnp.inf)
    row_max = jnp.max(scores, axis=-1, keepdims=True)
    weights = jnp.exp(scores - row_max)
    probabilities = (weights / jnp.sum(weights, axis=-1, keepdims=True)).astype(jnp.bfloat16)
    mixed = jnp.einsum(
        "hqk,hkd->hqd", probabilities, value_heads, preferred_element_type=jnp.float32
    )
    return mixed.astype(jnp.bfloat16)


def merge_rows(stream):
    feature_count = stream.shape[-1]
    shaped = stream.reshape(stream.shape[0] // (2 * PW), 2, PW // 2, 2, feature_count)
    return shaped.transpose(0, 2, 1, 3, 4).reshape(stream.shape[0] // 4, 4, feature_count)


def slot_ranks(owner_ids, group_total):
    owner_hits = (owner_ids[:, None] == jnp.arange(group_total, dtype=jnp.int32)[None, :]).astype(
        jnp.int32
    )
    before = jnp.cumsum(owner_hits, axis=0) - owner_hits
    return jnp.sum(before * owner_hits, axis=1)


def axis_exchange(value, axis_name):
    count = lax.axis_size(axis_name)
    got = [value]
    for shift in range(1, count):
        ring = [(i, (i + shift) % count) for i in range(count)]
        got.append(lax.ppermute(value, axis_name, ring))
    return got


def tp_gather(value, axis):
    count = lax.axis_size("tz")
    got = axis_exchange(value, "tz")
    mine = lax.axis_index("tz")
    blocks = []
    for k in range(count):
        which = (mine - k) % count
        block = got[0]
        for shift in range(1, count):
            block = jnp.where(which == shift, got[shift], block)
        blocks.append(block)
    inner = jnp.concatenate(blocks, axis=axis)
    return lax.all_gather(inner, "ty", axis=axis, tiled=True)


def exchange_sum(value):
    for axis_name in ("tz", "ty"):
        got = axis_exchange(value, axis_name)
        value = sum(got[1:], got[0])
    return value


def exchange_gather(value):
    for axis_name in ("tz", "ty"):
        value = jnp.concatenate(axis_exchange(value, axis_name), axis=0)
    return value


def tp_scatter_sum(value, axis):
    outer = lax.psum_scatter(value, "ty", scatter_dimension=axis, tiled=True)
    return lax.psum_scatter(outer, "tz", scatter_dimension=axis, tiled=True)


def scatter_sum_exchange(value, axis_name, axis):
    count = lax.axis_size(axis_name)
    shape = value.shape
    parts = value.reshape(shape[:axis] + (count, shape[axis] // count) + shape[axis + 1 :])
    got = lax.all_to_all(parts, axis_name, split_axis=axis, concat_axis=axis, tiled=True)
    return jnp.sum(got.astype(jnp.float32), axis=axis)


def butterfly_gather(value):
    out = value
    for axis_name in ("tz", "ty"):
        count = lax.axis_size(axis_name)
        step = 1
        while step < count:
            swap = [(i, i ^ step) for i in range(count)]
            out = jnp.concatenate([out, lax.ppermute(out, axis_name, swap)], axis=0)
            step = step * 2
    return out


def head_group_columns(weight):
    ty_count = lax.axis_size("ty")
    tz_count = lax.axis_size("tz")
    rows, cols = weight.shape
    width = cols // (ty_count * tz_count)
    parts = weight.reshape(1, rows, ty_count, tz_count, width)
    parts = lax.all_to_all(parts, "tz", split_axis=3, concat_axis=0, tiled=True)
    return parts.reshape(tz_count * rows, ty_count * width)


def req_exchange(outgoing):
    count = lax.axis_size("req")
    mine = lax.axis_index("req")
    ahead = jnp.roll(outgoing, -mine, axis=0)
    got = [ahead[0]]
    for shift in range(1, count):
        ring = [(i, (i + shift) % count) for i in range(count)]
        got.append(lax.ppermute(ahead[shift], "req", ring))
    ordered = jnp.stack([got[(count - k) % count] for k in range(count)], axis=0)
    return jnp.roll(ordered, mine, axis=0)


def per_device(
    tokens,
    segments,
    norm_gain,
    wqkv,
    qk_gain,
    wproj,
    bproj,
    layer_scale,
    ln_weight,
    ln_bias,
    w_merge,
    b_merge,
    owners,
):
    tp_total = lax.axis_size("ty") * lax.axis_size("tz")
    tp_index = lax.axis_index("ty") * lax.axis_size("tz") + lax.axis_index("tz")
    req_index = lax.axis_index("req")
    group_total = lax.axis_size("req")
    ln_rows = jnp.concatenate([ln_weight.reshape(1, -1), ln_bias.reshape(1, -1)], axis=0)
    ln_products = jnp.dot(
        ln_rows,
        w_merge.reshape(-1, w_merge.shape[2]),
        precision=lax.Precision.HIGHEST,
        preferred_element_type=jnp.float32,
    )
    gathered, wproj_group, ln_products = lax.optimization_barrier(
        (tp_gather(tokens, 1)[0], head_group_columns(wproj), ln_products)
    )
    gain_part = ln_products[0]
    bias_part = ln_products[1]
    seq_len = gathered.shape[0]
    group_segs = segments[0]
    widened = gathered.astype(jnp.float32)
    normed = (
        widened
        * lax.rsqrt(jnp.mean(widened * widened, axis=-1, keepdims=True) + EPS_RMS)
        * norm_gain
    ).astype(jnp.bfloat16)
    proj_qkv = jnp.einsum("td,ide->ite", normed, wqkv, preferred_element_type=jnp.float32)
    q_part = proj_qkv[0]
    k_part = proj_qkv[1]
    v_part = proj_qkv[2]
    square_sums = exchange_sum(
        jnp.stack([jnp.sum(q_part * q_part, axis=-1), jnp.sum(k_part * k_part, axis=-1)])
    )
    inner_width = HEADS * HD
    q_scaled = (
        q_part * lax.rsqrt(square_sums[0] / inner_width + EPS_RMS)[:, None] * qk_gain[0]
    ).astype(jnp.bfloat16)
    k_scaled = (
        k_part * lax.rsqrt(square_sums[1] / inner_width + EPS_RMS)[:, None] * qk_gain[1]
    ).astype(jnp.bfloat16)
    v_scaled = v_part.astype(jnp.bfloat16)
    heads_here = q_part.shape[1] // HD

    def split_heads(matrix):
        return matrix.reshape(seq_len, heads_here, HD).transpose(1, 0, 2)

    block_total = block_count(seq_len)
    block_rows = seq_len // block_total
    query_blocks = (
        split_heads(q_scaled).reshape(heads_here, block_total, block_rows, HD).transpose(1, 0, 2, 3)
    )
    seg_blocks = group_segs.reshape(block_total, block_rows)
    key_heads = split_heads(k_scaled)
    value_heads = split_heads(v_scaled)
    mixed = lax.map(
        lambda block_item: attend_block(
            block_item[0], key_heads, value_heads, block_item[1], group_segs
        ),
        (query_blocks, seg_blocks),
    )
    attended = mixed.transpose(0, 2, 1, 3).reshape(seq_len, heads_here * HD)
    width_dev = bproj.shape[0]
    group_heads = lax.all_gather(attended, "tz", axis=1, tiled=True)
    group_part = jnp.dot(group_heads, wproj_group, preferred_element_type=jnp.float32)
    attn_out = scatter_sum_exchange(group_part.astype(jnp.bfloat16), "ty", 1)
    own_columns = lax.dynamic_slice_in_dim(gathered, tp_index * width_dev, width_dev, 1).astype(
        jnp.float32
    )
    stream = (own_columns + layer_scale * (attn_out + bproj)).astype(jnp.bfloat16)
    merged = merge_rows(stream).astype(jnp.float32)
    feature_total = 4 * D
    local_count = 4 * width_dev
    local_sum = jnp.sum(merged, axis=(1, 2))
    local_mean = local_sum / local_count
    local_dev = merged - local_mean[:, None, None]
    local_m2 = jnp.sum(local_dev * local_dev, axis=(1, 2))
    merged_total = merged.shape[0]
    flat_weight = w_merge.reshape(4 * width_dev, w_merge.shape[2])
    local_rows = (local_dev * ln_weight).astype(jnp.bfloat16).reshape(merged_total, 4 * width_dev)
    local_part = lax.optimization_barrier(
        jnp.dot(local_rows, flat_weight, preferred_element_type=jnp.float32)
    )
    stats = exchange_gather(jnp.stack([local_sum, local_m2])[None])
    row_mean = jnp.sum(stats[:, 0], axis=0) / feature_total
    spread = stats[:, 0] / local_count - row_mean[None, :]
    row_m2 = jnp.sum(stats[:, 1], axis=0) + local_count * jnp.sum(spread * spread, axis=0)
    row_var = row_m2 / feature_total
    row_scale = lax.rsqrt(row_var + EPS_LN)
    shift = local_mean - row_mean
    row_part = (
        row_scale[:, None] * (local_part + shift[:, None] * gain_part[None, :]) + bias_part[None, :]
    )
    merged_dev = merged_total // tp_total
    row_outer = scatter_sum_exchange(row_part.astype(jnp.bfloat16), "ty", 0)
    own_rows = scatter_sum_exchange(row_outer.astype(jnp.bfloat16), "tz", 0)
    first_tokens = merge_rows(group_segs.reshape(seq_len, 1))[:, 0, 0]
    own_first = lax.dynamic_slice_in_dim(first_tokens, tp_index * merged_dev, merged_dev, 0)
    live_rows = (own_first >= 0).astype(jnp.float32)
    out_rows = (jax.nn.gelu(own_rows + b_merge, approximate=False) * live_rows[:, None]).astype(
        jnp.bfloat16
    )
    capacity = (merged_dev + group_total - 1) // group_total + 1
    group_ids = jnp.arange(group_total, dtype=jnp.int32)
    slot_ids = jnp.arange(capacity, dtype=jnp.int32)
    mine_ids = lax.dynamic_index_in_dim(owners[:, :, 0], req_index, 0, keepdims=False)
    slot_rank = slot_ranks(mine_ids, group_total)
    selector = (mine_ids[None, None, :] == group_ids[:, None, None]) & (
        slot_rank[None, None, :] == slot_ids[None, :, None]
    )
    outgoing = jnp.einsum(
        "gcm,mf->gcf", selector.astype(jnp.bfloat16), out_rows, preferred_element_type=jnp.float32
    ).astype(jnp.bfloat16)
    incoming = lax.all_to_all(outgoing, "req", split_axis=0, concat_axis=0, tiled=True)
    return incoming.reshape(1, group_total, 1, capacity, incoming.shape[-1])


def solution(mesh):
    grid = mesh.devices
    inner = 4 if grid.shape[1] % 4 == 0 else 1
    split = Mesh(
        grid.reshape(grid.shape[0], grid.shape[1] // inner, inner), ("req",) + TP_AXES
    )
    tp = TP_AXES
    placed = (
        P("req", tp, None),
        P("req", None),
        P(),
        P(None, None, tp),
        P(None, tp),
        P(tp, None),
        P(tp),
        P(tp),
        P(None, tp),
        P(None, tp),
        P(None, tp, None),
        P(),
        P(None, tp, None),
    )
    return jax.shard_map(
        per_device,
        mesh=split,
        in_specs=placed,
        out_specs=P("req", None, tp, None, None),
        check_vma=False,
    )
```

```python
import jax
import jax.numpy as jnp
from jax import lax
from jax.sharding import Mesh
from jax.sharding import PartitionSpec as P

D = 3200
HEADS = 16
HD = 128
PW = 32


EPS_RMS = 1e-06
EPS_LN = 1e-05

TP_AXES = ("ty", "tz")


def block_count(length):
    number = max(1, length // 512)
    while length % number:
        number = number - 1
    return number


def attend_block(query_rows, key_heads, value_heads, query_segs, key_segs):
    scores = jnp.einsum(
        "hqd,hkd->hqk", query_rows, key_heads, preferred_element_type=jnp.float32
    ) * HD ** (-0.5)
    same_image = query_segs[:, None] == key_segs[None, :]
    scores = jnp.where(same_image[None], scores, -jnp.inf)
    row_max = jnp.max(scores, axis=-1, keepdims=True)
    weights = jnp.exp(scores - row_max)
    probabilities = (weights / jnp.sum(weights, axis=-1, keepdims=True)).astype(jnp.bfloat16)
    mixed = jnp.einsum(
        "hqk,hkd->hqd", probabilities, value_heads, preferred_element_type=jnp.float32
    )
    return mixed.astype(jnp.bfloat16)


def merge_rows(stream):
    feature_count = stream.shape[-1]
    shaped = stream.reshape(stream.shape[0] // (2 * PW), 2, PW // 2, 2, feature_count)
    return shaped.transpose(0, 2, 1, 3, 4).reshape(stream.shape[0] // 4, 4, feature_count)


def slot_ranks(owner_ids, group_total):
    owner_hits = (owner_ids[:, None] == jnp.arange(group_total, dtype=jnp.int32)[None, :]).astype(
        jnp.int32
    )
    before = jnp.cumsum(owner_hits, axis=0) - owner_hits
    return jnp.sum(before * owner_hits, axis=1)


def axis_exchange(value, axis_name):
    count = lax.axis_size(axis_name)
    got = [value]
    for shift in range(1, count):
        ring = [(i, (i + shift) % count) for i in range(count)]
        got.append(lax.ppermute(value, axis_name, ring))
    return got


def tp_gather(value, axis):
    count = lax.axis_size("tz")
    got = axis_exchange(value, "tz")
    mine = lax.axis_index("tz")
    blocks = []
    for k in range(count):
        which = (mine - k) % count
        block = got[0]
        for shift in range(1, count):
            block = jnp.where(which == shift, got[shift], block)
        blocks.append(block)
    inner = jnp.concatenate(blocks, axis=axis)
    outer = axis_copies(inner, "ty")
    return jnp.concatenate([outer[k] for k in range(outer.shape[0])], axis=axis)


def axis_copies(value, axis_name):
    count = lax.axis_size(axis_name)
    copies = jnp.broadcast_to(value[None], (count,) + value.shape)
    return lax.all_to_all(copies, axis_name, split_axis=0, concat_axis=0, tiled=True)


def exchange_sum(value):
    for axis_name in ("tz", "ty"):
        got = axis_exchange(value, axis_name)
        value = sum(got[1:], got[0])
    return value


def exchange_gather(value):
    for axis_name in ("tz", "ty"):
        value = jnp.concatenate(axis_exchange(value, axis_name), axis=0)
    return value


def tp_scatter_sum(value, axis):
    outer = lax.psum_scatter(value, "ty", scatter_dimension=axis, tiled=True)
    return lax.psum_scatter(outer, "tz", scatter_dimension=axis, tiled=True)


def scatter_sum_exchange(value, axis_name, axis):
    count = lax.axis_size(axis_name)
    shape = value.shape
    parts = value.reshape(shape[:axis] + (count, shape[axis] // count) + shape[axis + 1 :])
    got = lax.all_to_all(parts, axis_name, split_axis=axis, concat_axis=axis, tiled=True)
    return jnp.sum(got.astype(jnp.float32), axis=axis)


def butterfly_gather(value):
    out = value
    for axis_name in ("tz", "ty"):
        count = lax.axis_size(axis_name)
        step = 1
        while step < count:
            swap = [(i, i ^ step) for i in range(count)]
            out = jnp.concatenate([out, lax.ppermute(out, axis_name, swap)], axis=0)
            step = step * 2
    return out


def head_group_columns(weight):
    ty_count = lax.axis_size("ty")
    tz_count = lax.axis_size("tz")
    rows, cols = weight.shape
    width = cols // (ty_count * tz_count)
    parts = weight.reshape(1, rows, ty_count, tz_count, width)
    parts = lax.all_to_all(parts, "tz", split_axis=3, concat_axis=0, tiled=True)
    return parts.reshape(tz_count * rows, ty_count * width)


def req_exchange(outgoing):
    count = lax.axis_size("req")
    mine = lax.axis_index("req")
    ahead = jnp.roll(outgoing, -mine, axis=0)
    got = [ahead[0]]
    for shift in range(1, count):
        ring = [(i, (i + shift) % count) for i in range(count)]
        got.append(lax.ppermute(ahead[shift], "req", ring))
    ordered = jnp.stack([got[(count - k) % count] for k in range(count)], axis=0)
    return jnp.roll(ordered, mine, axis=0)


def per_device(
    tokens,
    segments,
    norm_gain,
    wqkv,
    qk_gain,
    wproj,
    bproj,
    layer_scale,
    ln_weight,
    ln_bias,
    w_merge,
    b_merge,
    owners,
):
    tp_total = lax.axis_size("ty") * lax.axis_size("tz")
    tp_index = lax.axis_index("ty") * lax.axis_size("tz") + lax.axis_index("tz")
    req_index = lax.axis_index("req")
    group_total = lax.axis_size("req")
    ln_rows = jnp.concatenate([ln_weight.reshape(1, -1), ln_bias.reshape(1, -1)], axis=0)
    ln_products = jnp.dot(
        ln_rows,
        w_merge.reshape(-1, w_merge.shape[2]),
        precision=lax.Precision.HIGHEST,
        preferred_element_type=jnp.float32,
    )
    gathered, wproj_group, ln_products = lax.optimization_barrier(
        (tp_gather(tokens, 1)[0], head_group_columns(wproj), ln_products)
    )
    gain_part = ln_products[0]
    bias_part = ln_products[1]
    seq_len = gathered.shape[0]
    group_segs = segments[0]
    widened = gathered.astype(jnp.float32)
    normed = (
        widened
        * lax.rsqrt(jnp.mean(widened * widened, axis=-1, keepdims=True) + EPS_RMS)
        * norm_gain
    ).astype(jnp.bfloat16)
    proj_qkv = jnp.einsum("td,ide->ite", normed, wqkv, preferred_element_type=jnp.float32)
    q_part = proj_qkv[0]
    k_part = proj_qkv[1]
    v_part = proj_qkv[2]
    square_sums = exchange_sum(
        jnp.stack([jnp.sum(q_part * q_part, axis=-1), jnp.sum(k_part * k_part, axis=-1)])
    )
    inner_width = HEADS * HD
    q_scaled = (
        q_part * lax.rsqrt(square_sums[0] / inner_width + EPS_RMS)[:, None] * qk_gain[0]
    ).astype(jnp.bfloat16)
    k_scaled = (
        k_part * lax.rsqrt(square_sums[1] / inner_width + EPS_RMS)[:, None] * qk_gain[1]
    ).astype(jnp.bfloat16)
    v_scaled = v_part.astype(jnp.bfloat16)
    heads_here = q_part.shape[1] // HD

    def split_heads(matrix):
        return matrix.reshape(seq_len, heads_here, HD).transpose(1, 0, 2)

    block_total = block_count(seq_len)
    block_rows = seq_len // block_total
    query_blocks = (
        split_heads(q_scaled).reshape(heads_here, block_total, block_rows, HD).transpose(1, 0, 2, 3)
    )
    seg_blocks = group_segs.reshape(block_total, block_rows)
    key_heads = split_heads(k_scaled)
    value_heads = split_heads(v_scaled)
    mixed = lax.map(
        lambda block_item: attend_block(
            block_item[0], key_heads, value_heads, block_item[1], group_segs
        ),
        (query_blocks, seg_blocks),
    )
    attended = mixed.transpose(0, 2, 1, 3).reshape(seq_len, heads_here * HD)
    width_dev = bproj.shape[0]
    group_heads = lax.all_gather(attended, "tz", axis=1, tiled=True)
    group_part = jnp.dot(group_heads, wproj_group, preferred_element_type=jnp.float32)
    attn_out = scatter_sum_exchange(group_part.astype(jnp.bfloat16), "ty", 1)
    own_columns = lax.dynamic_slice_in_dim(gathered, tp_index * width_dev, width_dev, 1).astype(
        jnp.float32
    )
    stream = (own_columns + layer_scale * (attn_out + bproj)).astype(jnp.bfloat16)
    merged = merge_rows(stream).astype(jnp.float32)
    feature_total = 4 * D
    local_count = 4 * width_dev
    local_sum = jnp.sum(merged, axis=(1, 2))
    local_mean = local_sum / local_count
    local_dev = merged - local_mean[:, None, None]
    local_m2 = jnp.sum(local_dev * local_dev, axis=(1, 2))
    merged_total = merged.shape[0]
    flat_weight = w_merge.reshape(4 * width_dev, w_merge.shape[2])
    local_rows = (local_dev * ln_weight).astype(jnp.bfloat16).reshape(merged_total, 4 * width_dev)
    local_part = lax.optimization_barrier(
        jnp.dot(local_rows, flat_weight, preferred_element_type=jnp.float32)
    )
    stats = exchange_gather(jnp.stack([local_sum, local_m2])[None])
    row_mean = jnp.sum(stats[:, 0], axis=0) / feature_total
    spread = stats[:, 0] / local_count - row_mean[None, :]
    row_m2 = jnp.sum(stats[:, 1], axis=0) + local_count * jnp.sum(spread * spread, axis=0)
    row_var = row_m2 / feature_total
    row_scale = lax.rsqrt(row_var + EPS_LN)
    shift = local_mean - row_mean
    row_part = (
        row_scale[:, None] * (local_part + shift[:, None] * gain_part[None, :]) + bias_part[None, :]
    )
    merged_dev = merged_total // tp_total
    row_outer = scatter_sum_exchange(row_part.astype(jnp.bfloat16), "ty", 0)
    own_rows = scatter_sum_exchange(row_outer.astype(jnp.bfloat16), "tz", 0)
    first_tokens = merge_rows(group_segs.reshape(seq_len, 1))[:, 0, 0]
    own_first = lax.dynamic_slice_in_dim(first_tokens, tp_index * merged_dev, merged_dev, 0)
    live_rows = (own_first >= 0).astype(jnp.float32)
    out_rows = (jax.nn.gelu(own_rows + b_merge, approximate=False) * live_rows[:, None]).astype(
        jnp.bfloat16
    )
    capacity = (merged_dev + group_total - 1) // group_total + 1
    group_ids = jnp.arange(group_total, dtype=jnp.int32)
    slot_ids = jnp.arange(capacity, dtype=jnp.int32)
    mine_ids = lax.dynamic_index_in_dim(owners[:, :, 0], req_index, 0, keepdims=False)
    slot_rank = slot_ranks(mine_ids, group_total)
    selector = (mine_ids[None, None, :] == group_ids[:, None, None]) & (
        slot_rank[None, None, :] == slot_ids[None, :, None]
    )
    outgoing = jnp.einsum(
        "gcm,mf->gcf", selector.astype(jnp.bfloat16), out_rows, preferred_element_type=jnp.float32
    ).astype(jnp.bfloat16)
    incoming = lax.all_to_all(outgoing, "req", split_axis=0, concat_axis=0, tiled=True)
    return incoming.reshape(1, group_total, 1, capacity, incoming.shape[-1])


def solution(mesh):
    grid = mesh.devices
    inner = 4 if grid.shape[1] % 4 == 0 else 1
    split = Mesh(
        grid.reshape(grid.shape[0], grid.shape[1] // inner, inner), ("req",) + TP_AXES
    )
    tp = TP_AXES
    placed = (
        P("req", tp, None),
        P("req", None),
        P(),
        P(None, None, tp),
        P(None, tp),
        P(tp, None),
        P(tp),
        P(tp),
        P(None, tp),
        P(None, tp),
        P(None, tp, None),
        P(),
        P(None, tp, None),
    )
    return jax.shard_map(
        per_device,
        mesh=split,
        in_specs=placed,
        out_specs=P("req", None, tp, None, None),
        check_vma=False,
    )
```

```python
import jax
import jax.numpy as jnp
from jax import lax
from jax.sharding import Mesh
from jax.sharding import PartitionSpec as P

D = 3200
HEADS = 16
HD = 128
PW = 32


EPS_RMS = 1e-06
EPS_LN = 1e-05

TP_AXES = ("ty", "tz")


def block_count(length):
    number = max(1, length // 512)
    while length % number:
        number = number - 1
    return number


def attend_block(query_rows, key_heads, value_heads, query_segs, key_segs):
    scores = jnp.einsum(
        "hqd,hkd->hqk", query_rows, key_heads, preferred_element_type=jnp.float32
    ) * HD ** (-0.5)
    same_image = query_segs[:, None] == key_segs[None, :]
    scores = jnp.where(same_image[None], scores, -jnp.inf)
    row_max = jnp.max(scores, axis=-1, keepdims=True)
    weights = jnp.exp(scores - row_max)
    probabilities = (weights / jnp.sum(weights, axis=-1, keepdims=True)).astype(jnp.bfloat16)
    mixed = jnp.einsum(
        "hqk,hkd->hqd", probabilities, value_heads, preferred_element_type=jnp.float32
    )
    return mixed.astype(jnp.bfloat16)


def merge_rows(stream):
    feature_count = stream.shape[-1]
    shaped = stream.reshape(stream.shape[0] // (2 * PW), 2, PW // 2, 2, feature_count)
    return shaped.transpose(0, 2, 1, 3, 4).reshape(stream.shape[0] // 4, 4, feature_count)


def slot_ranks(owner_ids, group_total):
    owner_hits = (owner_ids[:, None] == jnp.arange(group_total, dtype=jnp.int32)[None, :]).astype(
        jnp.int32
    )
    before = jnp.cumsum(owner_hits, axis=0) - owner_hits
    return jnp.sum(before * owner_hits, axis=1)


def axis_exchange(value, axis_name):
    count = lax.axis_size(axis_name)
    got = [value]
    for shift in range(1, count):
        ring = [(i, (i + shift) % count) for i in range(count)]
        got.append(lax.ppermute(value, axis_name, ring))
    return got


def tp_gather(value, axis, weight):
    count = lax.axis_size("tz")
    got = axis_exchange(value, "tz")
    mine = lax.axis_index("tz")
    blocks = []
    for k in range(count):
        which = (mine - k) % count
        block = got[0]
        for shift in range(1, count):
            block = jnp.where(which == shift, got[shift], block)
        blocks.append(block)
    inner = jnp.concatenate(blocks, axis=axis)
    inner, weight = lax.optimization_barrier((inner, weight))
    outer = axis_copies(inner, "ty")
    gathered = jnp.concatenate([outer[k] for k in range(outer.shape[0])], axis=axis)
    return gathered, head_group_columns(weight)


def axis_copies(value, axis_name):
    count = lax.axis_size(axis_name)
    copies = jnp.broadcast_to(value[None], (count,) + value.shape)
    return lax.all_to_all(copies, axis_name, split_axis=0, concat_axis=0, tiled=True)


def exchange_sum(value):
    for axis_name in ("tz", "ty"):
        got = axis_exchange(value, axis_name)
        value = sum(got[1:], got[0])
    return value


def exchange_gather(value):
    for axis_name in ("tz", "ty"):
        value = jnp.concatenate(axis_exchange(value, axis_name), axis=0)
    return value


def tp_scatter_sum(value, axis):
    outer = lax.psum_scatter(value, "ty", scatter_dimension=axis, tiled=True)
    return lax.psum_scatter(outer, "tz", scatter_dimension=axis, tiled=True)


def scatter_sum_exchange(value, axis_name, axis):
    count = lax.axis_size(axis_name)
    shape = value.shape
    parts = value.reshape(shape[:axis] + (count, shape[axis] // count) + shape[axis + 1 :])
    got = lax.all_to_all(parts, axis_name, split_axis=axis, concat_axis=axis, tiled=True)
    return jnp.sum(got.astype(jnp.float32), axis=axis)


def butterfly_gather(value):
    out = value
    for axis_name in ("tz", "ty"):
        count = lax.axis_size(axis_name)
        step = 1
        while step < count:
            swap = [(i, i ^ step) for i in range(count)]
            out = jnp.concatenate([out, lax.ppermute(out, axis_name, swap)], axis=0)
            step = step * 2
    return out


def head_group_columns(weight):
    ty_count = lax.axis_size("ty")
    tz_count = lax.axis_size("tz")
    rows, cols = weight.shape
    width = cols // (ty_count * tz_count)
    parts = weight.reshape(1, rows, ty_count, tz_count, width)
    parts = lax.all_to_all(parts, "tz", split_axis=3, concat_axis=0, tiled=True)
    return parts.reshape(tz_count * rows, ty_count * width)


def req_exchange(outgoing):
    count = lax.axis_size("req")
    mine = lax.axis_index("req")
    ahead = jnp.roll(outgoing, -mine, axis=0)
    got = [ahead[0]]
    for shift in range(1, count):
        ring = [(i, (i + shift) % count) for i in range(count)]
        got.append(lax.ppermute(ahead[shift], "req", ring))
    ordered = jnp.stack([got[(count - k) % count] for k in range(count)], axis=0)
    return jnp.roll(ordered, mine, axis=0)


def per_device(
    tokens,
    segments,
    norm_gain,
    wqkv,
    qk_gain,
    wproj,
    bproj,
    layer_scale,
    ln_weight,
    ln_bias,
    w_merge,
    b_merge,
    owners,
):
    tp_total = lax.axis_size("ty") * lax.axis_size("tz")
    tp_index = lax.axis_index("ty") * lax.axis_size("tz") + lax.axis_index("tz")
    req_index = lax.axis_index("req")
    group_total = lax.axis_size("req")
    ln_rows = jnp.concatenate([ln_weight.reshape(1, -1), ln_bias.reshape(1, -1)], axis=0)
    ln_products = jnp.dot(
        ln_rows,
        w_merge.reshape(-1, w_merge.shape[2]),
        precision=lax.Precision.HIGHEST,
        preferred_element_type=jnp.float32,
    )
    gathered, wproj_group, ln_products = lax.optimization_barrier(
        tp_gather(tokens, 1, wproj) + (ln_products,)
    )
    gathered = gathered[0]
    gain_part = ln_products[0]
    bias_part = ln_products[1]
    seq_len = gathered.shape[0]
    group_segs = segments[0]
    widened = gathered.astype(jnp.float32)
    normed = (
        widened
        * lax.rsqrt(jnp.mean(widened * widened, axis=-1, keepdims=True) + EPS_RMS)
        * norm_gain
    ).astype(jnp.bfloat16)
    proj_qkv = jnp.einsum("td,ide->ite", normed, wqkv, preferred_element_type=jnp.float32)
    q_part = proj_qkv[0]
    k_part = proj_qkv[1]
    v_part = proj_qkv[2]
    square_sums = exchange_sum(
        jnp.stack([jnp.sum(q_part * q_part, axis=-1), jnp.sum(k_part * k_part, axis=-1)])
    )
    inner_width = HEADS * HD
    q_scaled = (
        q_part * lax.rsqrt(square_sums[0] / inner_width + EPS_RMS)[:, None] * qk_gain[0]
    ).astype(jnp.bfloat16)
    k_scaled = (
        k_part * lax.rsqrt(square_sums[1] / inner_width + EPS_RMS)[:, None] * qk_gain[1]
    ).astype(jnp.bfloat16)
    v_scaled = v_part.astype(jnp.bfloat16)
    heads_here = q_part.shape[1] // HD

    def split_heads(matrix):
        return matrix.reshape(seq_len, heads_here, HD).transpose(1, 0, 2)

    block_total = block_count(seq_len)
    block_rows = seq_len // block_total
    query_blocks = (
        split_heads(q_scaled).reshape(heads_here, block_total, block_rows, HD).transpose(1, 0, 2, 3)
    )
    seg_blocks = group_segs.reshape(block_total, block_rows)
    key_heads = split_heads(k_scaled)
    value_heads = split_heads(v_scaled)
    mixed = lax.map(
        lambda block_item: attend_block(
            block_item[0], key_heads, value_heads, block_item[1], group_segs
        ),
        (query_blocks, seg_blocks),
    )
    attended = mixed.transpose(0, 2, 1, 3).reshape(seq_len, heads_here * HD)
    width_dev = bproj.shape[0]
    group_heads = lax.all_gather(attended, "tz", axis=1, tiled=True)
    group_part = jnp.dot(group_heads, wproj_group, preferred_element_type=jnp.float32)
    attn_out = scatter_sum_exchange(group_part.astype(jnp.bfloat16), "ty", 1)
    own_columns = lax.dynamic_slice_in_dim(gathered, tp_index * width_dev, width_dev, 1).astype(
        jnp.float32
    )
    stream = (own_columns + layer_scale * (attn_out + bproj)).astype(jnp.bfloat16)
    merged = merge_rows(stream).astype(jnp.float32)
    feature_total = 4 * D
    local_count = 4 * width_dev
    local_sum = jnp.sum(merged, axis=(1, 2))
    local_mean = local_sum / local_count
    local_dev = merged - local_mean[:, None, None]
    local_m2 = jnp.sum(local_dev * local_dev, axis=(1, 2))
    merged_total = merged.shape[0]
    flat_weight = w_merge.reshape(4 * width_dev, w_merge.shape[2])
    local_rows = (local_dev * ln_weight).astype(jnp.bfloat16).reshape(merged_total, 4 * width_dev)
    local_part = lax.optimization_barrier(
        jnp.dot(local_rows, flat_weight, preferred_element_type=jnp.float32)
    )
    stats = exchange_gather(jnp.stack([local_sum, local_m2])[None])
    row_mean = jnp.sum(stats[:, 0], axis=0) / feature_total
    spread = stats[:, 0] / local_count - row_mean[None, :]
    row_m2 = jnp.sum(stats[:, 1], axis=0) + local_count * jnp.sum(spread * spread, axis=0)
    row_var = row_m2 / feature_total
    row_scale = lax.rsqrt(row_var + EPS_LN)
    shift = local_mean - row_mean
    row_part = (
        row_scale[:, None] * (local_part + shift[:, None] * gain_part[None, :]) + bias_part[None, :]
    )
    merged_dev = merged_total // tp_total
    row_outer = scatter_sum_exchange(row_part.astype(jnp.bfloat16), "ty", 0)
    own_rows = scatter_sum_exchange(row_outer.astype(jnp.bfloat16), "tz", 0)
    first_tokens = merge_rows(group_segs.reshape(seq_len, 1))[:, 0, 0]
    own_first = lax.dynamic_slice_in_dim(first_tokens, tp_index * merged_dev, merged_dev, 0)
    live_rows = (own_first >= 0).astype(jnp.float32)
    out_rows = (jax.nn.gelu(own_rows + b_merge, approximate=False) * live_rows[:, None]).astype(
        jnp.bfloat16
    )
    capacity = (merged_dev + group_total - 1) // group_total + 1
    group_ids = jnp.arange(group_total, dtype=jnp.int32)
    slot_ids = jnp.arange(capacity, dtype=jnp.int32)
    mine_ids = lax.dynamic_index_in_dim(owners[:, :, 0], req_index, 0, keepdims=False)
    slot_rank = slot_ranks(mine_ids, group_total)
    selector = (mine_ids[None, None, :] == group_ids[:, None, None]) & (
        slot_rank[None, None, :] == slot_ids[None, :, None]
    )
    outgoing = jnp.einsum(
        "gcm,mf->gcf", selector.astype(jnp.bfloat16), out_rows, preferred_element_type=jnp.float32
    ).astype(jnp.bfloat16)
    incoming = lax.all_to_all(outgoing, "req", split_axis=0, concat_axis=0, tiled=True)
    return incoming.reshape(1, group_total, 1, capacity, incoming.shape[-1])


def solution(mesh):
    grid = mesh.devices
    inner = 4 if grid.shape[1] % 4 == 0 else 1
    split = Mesh(
        grid.reshape(grid.shape[0], grid.shape[1] // inner, inner), ("req",) + TP_AXES
    )
    tp = TP_AXES
    placed = (
        P("req", tp, None),
        P("req", None),
        P(),
        P(None, None, tp),
        P(None, tp),
        P(tp, None),
        P(tp),
        P(tp),
        P(None, tp),
        P(None, tp),
        P(None, tp, None),
        P(),
        P(None, tp, None),
    )
    return jax.shard_map(
        per_device,
        mesh=split,
        in_specs=placed,
        out_specs=P("req", None, tp, None, None),
        check_vma=False,
    )
```

```python
import jax
import jax.numpy as jnp
from jax import lax
from jax.sharding import Mesh
from jax.sharding import PartitionSpec as P

D = 3200
HEADS = 16
HD = 128
PW = 32


EPS_RMS = 1e-06
EPS_LN = 1e-05

TP_AXES = ("ty", "tz")


def block_count(length):
    number = max(1, length // 512)
    while length % number:
        number = number - 1
    return number


def attend_block(query_rows, key_heads, value_heads, query_segs, key_segs):
    scores = jnp.einsum(
        "hqd,hkd->hqk", query_rows, key_heads, preferred_element_type=jnp.float32
    ) * HD ** (-0.5)
    same_image = query_segs[:, None] == key_segs[None, :]
    scores = jnp.where(same_image[None], scores, -jnp.inf)
    row_max = jnp.max(scores, axis=-1, keepdims=True)
    weights = jnp.exp(scores - row_max)
    probabilities = (weights / jnp.sum(weights, axis=-1, keepdims=True)).astype(jnp.bfloat16)
    mixed = jnp.einsum(
        "hqk,hkd->hqd", probabilities, value_heads, preferred_element_type=jnp.float32
    )
    return mixed.astype(jnp.bfloat16)


def merge_rows(stream):
    feature_count = stream.shape[-1]
    shaped = stream.reshape(stream.shape[0] // (2 * PW), 2, PW // 2, 2, feature_count)
    return shaped.transpose(0, 2, 1, 3, 4).reshape(stream.shape[0] // 4, 4, feature_count)


def slot_ranks(owner_ids, group_total):
    owner_hits = (owner_ids[:, None] == jnp.arange(group_total, dtype=jnp.int32)[None, :]).astype(
        jnp.int32
    )
    before = jnp.cumsum(owner_hits, axis=0) - owner_hits
    return jnp.sum(before * owner_hits, axis=1)


def axis_exchange(value, axis_name):
    count = lax.axis_size(axis_name)
    got = [value]
    for shift in range(1, count):
        ring = [(i, (i + shift) % count) for i in range(count)]
        got.append(lax.ppermute(value, axis_name, ring))
    return got


def tp_gather(value, axis):
    count = lax.axis_size("tz")
    got = axis_exchange(value, "tz")
    mine = lax.axis_index("tz")
    blocks = []
    for k in range(count):
        which = (mine - k) % count
        block = got[0]
        for shift in range(1, count):
            block = jnp.where(which == shift, got[shift], block)
        blocks.append(block)
    inner = jnp.concatenate(blocks, axis=axis)
    outer = axis_copies(inner, "ty")
    return jnp.concatenate([outer[k] for k in range(outer.shape[0])], axis=axis)


def axis_copies(value, axis_name):
    count = lax.axis_size(axis_name)
    copies = jnp.broadcast_to(value[None], (count,) + value.shape)
    return lax.all_to_all(copies, axis_name, split_axis=0, concat_axis=0, tiled=True)


def exchange_sum(value):
    for axis_name in ("tz", "ty"):
        got = axis_exchange(value, axis_name)
        value = sum(got[1:], got[0])
    return value


def exchange_gather(value):
    for axis_name in ("tz", "ty"):
        value = jnp.concatenate(axis_exchange(value, axis_name), axis=0)
    return value


def tp_scatter_sum(value, axis):
    outer = lax.psum_scatter(value, "ty", scatter_dimension=axis, tiled=True)
    return lax.psum_scatter(outer, "tz", scatter_dimension=axis, tiled=True)


def scatter_sum_exchange(value, axis_name, axis):
    count = lax.axis_size(axis_name)
    shape = value.shape
    parts = value.reshape(shape[:axis] + (count, shape[axis] // count) + shape[axis + 1 :])
    got = lax.all_to_all(parts, axis_name, split_axis=axis, concat_axis=axis, tiled=True)
    return jnp.sum(got.astype(jnp.float32), axis=axis)


def butterfly_gather(value):
    out = value
    for axis_name in ("tz", "ty"):
        count = lax.axis_size(axis_name)
        step = 1
        while step < count:
            swap = [(i, i ^ step) for i in range(count)]
            out = jnp.concatenate([out, lax.ppermute(out, axis_name, swap)], axis=0)
            step = step * 2
    return out


def head_group_columns(weight):
    ty_count = lax.axis_size("ty")
    tz_count = lax.axis_size("tz")
    rows, cols = weight.shape
    width = cols // (ty_count * tz_count)
    parts = weight.reshape(1, rows, ty_count, tz_count, width)
    parts = lax.all_to_all(parts, "tz", split_axis=3, concat_axis=0, tiled=True)
    return parts.reshape(tz_count * rows, ty_count * width)


def req_exchange(outgoing):
    count = lax.axis_size("req")
    mine = lax.axis_index("req")
    ahead = jnp.roll(outgoing, -mine, axis=0)
    got = [ahead[0]]
    for shift in range(1, count):
        ring = [(i, (i + shift) % count) for i in range(count)]
        got.append(lax.ppermute(ahead[shift], "req", ring))
    ordered = jnp.stack([got[(count - k) % count] for k in range(count)], axis=0)
    return jnp.roll(ordered, mine, axis=0)


def per_device(
    tokens,
    segments,
    norm_gain,
    wqkv,
    qk_gain,
    wproj,
    bproj,
    layer_scale,
    ln_weight,
    ln_bias,
    w_merge,
    b_merge,
    owners,
):
    tp_total = lax.axis_size("ty") * lax.axis_size("tz")
    tp_index = lax.axis_index("ty") * lax.axis_size("tz") + lax.axis_index("tz")
    req_index = lax.axis_index("req")
    group_total = lax.axis_size("req")
    ln_rows = jnp.concatenate([ln_weight.reshape(1, -1), ln_bias.reshape(1, -1)], axis=0)
    ln_products = jnp.dot(
        ln_rows,
        w_merge.reshape(-1, w_merge.shape[2]),
        precision=lax.Precision.HIGHEST,
        preferred_element_type=jnp.float32,
    )
    gathered, wproj_group, ln_products = lax.optimization_barrier(
        (tp_gather(tokens, 1)[0], head_group_columns(wproj), ln_products)
    )
    gain_part = ln_products[0]
    bias_part = ln_products[1]
    seq_len = gathered.shape[0]
    group_segs = segments[0]
    widened = gathered.astype(jnp.float32)
    normed = (
        widened
        * lax.rsqrt(jnp.mean(widened * widened, axis=-1, keepdims=True) + EPS_RMS)
        * norm_gain
    ).astype(jnp.bfloat16)
    proj_qk = jnp.einsum("td,ide->ite", normed, wqkv[:2], preferred_element_type=jnp.float32)
    q_part = proj_qk[0]
    k_part = proj_qk[1]
    v_part = jnp.dot(normed, wqkv[2], preferred_element_type=jnp.float32)
    square_sums = exchange_sum(
        jnp.stack([jnp.sum(q_part * q_part, axis=-1), jnp.sum(k_part * k_part, axis=-1)])
    )
    inner_width = HEADS * HD
    q_scaled = (
        q_part * lax.rsqrt(square_sums[0] / inner_width + EPS_RMS)[:, None] * qk_gain[0]
    ).astype(jnp.bfloat16)
    k_scaled = (
        k_part * lax.rsqrt(square_sums[1] / inner_width + EPS_RMS)[:, None] * qk_gain[1]
    ).astype(jnp.bfloat16)
    v_scaled = v_part.astype(jnp.bfloat16)
    heads_here = q_part.shape[1] // HD

    def split_heads(matrix):
        return matrix.reshape(seq_len, heads_here, HD).transpose(1, 0, 2)

    block_total = block_count(seq_len)
    block_rows = seq_len // block_total
    query_blocks = (
        split_heads(q_scaled).reshape(heads_here, block_total, block_rows, HD).transpose(1, 0, 2, 3)
    )
    seg_blocks = group_segs.reshape(block_total, block_rows)
    key_heads = split_heads(k_scaled)
    value_heads = split_heads(v_scaled)
    mixed = lax.map(
        lambda block_item: attend_block(
            block_item[0], key_heads, value_heads, block_item[1], group_segs
        ),
        (query_blocks, seg_blocks),
    )
    attended = mixed.transpose(0, 2, 1, 3).reshape(seq_len, heads_here * HD)
    width_dev = bproj.shape[0]
    group_heads = lax.all_gather(attended, "tz", axis=1, tiled=True)
    group_part = jnp.dot(group_heads, wproj_group, preferred_element_type=jnp.float32)
    attn_out = scatter_sum_exchange(group_part.astype(jnp.bfloat16), "ty", 1)
    own_columns = lax.dynamic_slice_in_dim(gathered, tp_index * width_dev, width_dev, 1).astype(
        jnp.float32
    )
    stream = (own_columns + layer_scale * (attn_out + bproj)).astype(jnp.bfloat16)
    merged = merge_rows(stream).astype(jnp.float32)
    feature_total = 4 * D
    local_count = 4 * width_dev
    local_sum = jnp.sum(merged, axis=(1, 2))
    local_mean = local_sum / local_count
    local_dev = merged - local_mean[:, None, None]
    local_m2 = jnp.sum(local_dev * local_dev, axis=(1, 2))
    merged_total = merged.shape[0]
    flat_weight = w_merge.reshape(4 * width_dev, w_merge.shape[2])
    local_rows = (local_dev * ln_weight).astype(jnp.bfloat16).reshape(merged_total, 4 * width_dev)
    local_part = lax.optimization_barrier(
        jnp.dot(local_rows, flat_weight, preferred_element_type=jnp.float32)
    )
    stats = exchange_gather(jnp.stack([local_sum, local_m2])[None])
    row_mean = jnp.sum(stats[:, 0], axis=0) / feature_total
    spread = stats[:, 0] / local_count - row_mean[None, :]
    row_m2 = jnp.sum(stats[:, 1], axis=0) + local_count * jnp.sum(spread * spread, axis=0)
    row_var = row_m2 / feature_total
    row_scale = lax.rsqrt(row_var + EPS_LN)
    shift = local_mean - row_mean
    row_part = (
        row_scale[:, None] * (local_part + shift[:, None] * gain_part[None, :]) + bias_part[None, :]
    )
    merged_dev = merged_total // tp_total
    row_outer = scatter_sum_exchange(row_part.astype(jnp.bfloat16), "ty", 0)
    own_rows = scatter_sum_exchange(row_outer.astype(jnp.bfloat16), "tz", 0)
    first_tokens = merge_rows(group_segs.reshape(seq_len, 1))[:, 0, 0]
    own_first = lax.dynamic_slice_in_dim(first_tokens, tp_index * merged_dev, merged_dev, 0)
    live_rows = (own_first >= 0).astype(jnp.float32)
    out_rows = (jax.nn.gelu(own_rows + b_merge, approximate=False) * live_rows[:, None]).astype(
        jnp.bfloat16
    )
    capacity = (merged_dev + group_total - 1) // group_total + 1
    group_ids = jnp.arange(group_total, dtype=jnp.int32)
    slot_ids = jnp.arange(capacity, dtype=jnp.int32)
    mine_ids = lax.dynamic_index_in_dim(owners[:, :, 0], req_index, 0, keepdims=False)
    slot_rank = slot_ranks(mine_ids, group_total)
    selector = (mine_ids[None, None, :] == group_ids[:, None, None]) & (
        slot_rank[None, None, :] == slot_ids[None, :, None]
    )
    outgoing = jnp.einsum(
        "gcm,mf->gcf", selector.astype(jnp.bfloat16), out_rows, preferred_element_type=jnp.float32
    ).astype(jnp.bfloat16)
    incoming = lax.all_to_all(outgoing, "req", split_axis=0, concat_axis=0, tiled=True)
    return incoming.reshape(1, group_total, 1, capacity, incoming.shape[-1])


def solution(mesh):
    grid = mesh.devices
    inner = 4 if grid.shape[1] % 4 == 0 else 1
    split = Mesh(
        grid.reshape(grid.shape[0], grid.shape[1] // inner, inner), ("req",) + TP_AXES
    )
    tp = TP_AXES
    placed = (
        P("req", tp, None),
        P("req", None),
        P(),
        P(None, None, tp),
        P(None, tp),
        P(tp, None),
        P(tp),
        P(tp),
        P(None, tp),
        P(None, tp),
        P(None, tp, None),
        P(),
        P(None, tp, None),
    )
    return jax.shard_map(
        per_device,
        mesh=split,
        in_specs=placed,
        out_specs=P("req", None, tp, None, None),
        check_vma=False,
    )
```
